32 devices in a mesh: tm: 8 (over z, x), ens: 4 (over y, core).
Axes of the slice: x: 2, y: 2, z: 4, core: 2. Of those that a mesh axis runs over, the one named last changes fastest.
Arguments:
- readings: float32 [128, 1024], P('tm', 'ens'), parts along dimension 1, may hold values from -6 to 6
- seen_mask: int32 [128, 256], P('tm'), may hold values 0 or 1
- sensor: int32 [128], P('tm'), may hold values from 0 to 3
- time_gaps: float32 [128], replicated, may hold values from 0.49 to 89.6, as said below
- noise_var: float32 [4, 1024], P(None, 'ens'), parts along dimension 1, may hold values from 0.05 to 0.5
- readout: float32 [4, 1024], P(None, 'ens'), parts along dimension 1, may hold values from -4 to 4
- angles: float32 [4, 1024], P(None, 'ens'), parts along dimension 1, may hold values from -3.140625 to 3.140625
- decay_rates: float32 [1024], P('ens'), parts along dimension 0, may hold values from 0.000703125 to 0.034, as said below
- field_cov: float32 [4, 4, 1024], P(None, None, 'ens'), parts along dimension 2, as said below
Outputs:
- smoothed_mean: float32 [128, 4, 1024], P('tm', None, 'ens'), parts along dimension 2
- log_spread: float32 [128, 1024], P('tm', 'ens'), parts along dimension 1
The draws below stay inside these ranges and needn't reach their ends.
There are 4 independent parts, one for each index of `ens`. The reference program is written for one: setup_inputs(seed, part) draws one part's arguments, and reference() takes and returns one part's arrays. A program takes and returns all parts, laid end to end along the dimension named above; an argument that names none is the same for every part. Nothing has to cross between parts.
Inputs may be any that keep to these rules, and one draw needn't show every extreme that they name: `time_gaps`: positive time gaps. `decay_rates`: positive rates. `field_cov`: symmetric, with a dominant positive diagonal.
All inputs are finite; a program needn't handle non-finite values. No bound on the sum of `seen_mask` on one device may be relied on, other than what follows from the above.
Results may differ from the reference program's by a relative error of at most 0.0003.
Values sent between devices are 32-bit elements; how exact they have to be, the bound alone decides.
No kernel may reach another device: no remote copies, remote signals or barrier semaphores. Data moves between devices by JAX's collectives and lax.ppermute only.
A program may use at most 64 MiB of HBM per device.

```python
import math
import jax
import jax.numpy as jnp
from jax import lax

MODES = 256
ORDER = 4
INSTR = 4
TIMES = 128


def draw_decay_rates(key, part):
    pick_key, slow_key, fast_key = jax.random.split(jax.random.fold_in(key, 11), 3)
    slow_share = 0.5
    chooser = jax.random.uniform(pick_key, (MODES,), dtype=jnp.float32)
    slow_rate = jnp.exp(jax.random.uniform(slow_key, (MODES,), dtype=jnp.float32, minval=math.log(0.1 / TIMES), maxval=math.log(0.7 / TIMES)))
    fast_rate = jnp.exp(jax.random.uniform(fast_key, (MODES,), dtype=jnp.float32, minval=math.log(1.0 / 50.0), maxval=math.log(1.0 / 30.0)))
    return jnp.where(chooser < slow_share, slow_rate, fast_rate).astype(jnp.float32)


def draw_time_gaps(key, part):
    regular_key, place_key, length_key = jax.random.split(jax.random.fold_in(key, 23), 3)
    regular = jnp.exp(jax.random.uniform(regular_key, (TIMES,), dtype=jnp.float32, minval=math.log(0.5), maxval=math.log(2.0)))
    outage_at = jax.random.randint(place_key, (4,), 1, TIMES)
    outage = TIMES * jax.random.uniform(length_key, (4,), dtype=jnp.float32, minval=0.25, maxval=0.7)
    return regular.at[outage_at].set(outage).astype(jnp.float32)


def draw_field_cov(key, part):
    off_key, diag_key, scale_key = jax.random.split(jax.random.fold_in(key, 37), 3)
    raw_off = jax.random.uniform(off_key, (ORDER, ORDER, MODES), dtype=jnp.float32, minval=-0.3, maxval=0.3)
    symmetric = 0.5 * (raw_off + jnp.swapaxes(raw_off, 0, 1))
    diagonal = jax.random.uniform(diag_key, (ORDER, MODES), dtype=jnp.float32, minval=1.0, maxval=2.0)
    scale_low = 0.3
    scale_high = 3.0
    scaling = jnp.exp(jax.random.uniform(scale_key, (MODES,), dtype=jnp.float32, minval=math.log(scale_low), maxval=math.log(scale_high)))
    identity = jnp.eye(ORDER, dtype=jnp.float32)[:, :, None]
    result = (symmetric * (1.0 - identity) + identity * diagonal[:, None, :]) * scaling[None, None, :]
    return result.astype(jnp.float32)


def set_ends(values, key, low, largest):
    longest = values.shape.index(max(values.shape))
    spots = []
    for shift in (0, 1):
        where = [jax.random.randint(jax.random.fold_in(key, axis), (), 0, length) for axis, length in enumerate(values.shape)]
        where[longest] = (where[longest] + shift) % values.shape[longest]
        spots.append(tuple(where))
    return values.at[spots[0]].set(low).at[spots[1]].set(largest)


def levels(rng, dims, pieces, least, high):
    level, own = 1.0, jax.random.fold_in(rng, 6)
    for dim, shards_of in pieces:
        draws = jnp.exp(jax.random.uniform(jax.random.fold_in(own, dim), (shards_of,), jnp.float32, least / len(pieces), high / len(pieces)))
        level = level * jnp.repeat(draws, dims[dim] // shards_of).reshape([-1 if axis == dim else 1 for axis in range(len(dims))])
    return level


def gaussian(own_key, dims, deviation, most, pieces=(), kind=jnp.bfloat16):
    loudness = levels(own_key, dims, pieces, -0.22, 0.18) if pieces else 1.0
    array = jax.random.normal(own_key, dims, jnp.float32) * deviation * loudness
    return jnp.minimum(jnp.maximum(array, -most), most).astype(kind)


def setup_inputs(seed: int = 0, part: int = 0) -> dict:
    key_list = jax.random.split(jax.random.key(seed), 10)
    part_splits = jax.random.split(jax.random.fold_in(key_list[9], part), 10)
    return {
        "readings": gaussian(part_splits[0], (TIMES, MODES), 1.0, 6.0, ((0, 8),), jnp.float32),
        "seen_mask": set_ends((jax.random.randint(key_list[1], (TIMES, MODES), 0, 4) < 3).astype(jnp.int32), jax.random.fold_in(key_list[1], 1), 0, 1),
        "sensor": set_ends(jax.random.randint(key_list[2], (TIMES,), 0, INSTR), jax.random.fold_in(key_list[2], 1), 0, INSTR - 1).astype(jnp.int32),
        "time_gaps": draw_time_gaps(jax.random.fold_in(key_list[9], 71), part),
        "noise_var": jnp.clip(jnp.exp(jax.random.uniform(part_splits[4], (INSTR, MODES), jnp.float32, math.log(0.05), math.log(0.5))), 0.05, 0.5),
        "readout": gaussian(part_splits[5], (ORDER, MODES), 0.6, 4.0, (), jnp.float32),
        "angles": jnp.clip(jax.random.uniform(part_splits[6], (ORDER, MODES), jnp.float32, -3.140625, 3.140625), -3.140625, 3.140625),
        "decay_rates": draw_decay_rates(jax.random.fold_in(jax.random.fold_in(key_list[9], part), 71), part),
        "field_cov": draw_field_cov(jax.random.fold_in(jax.random.fold_in(key_list[9], part), 71), part),
    }


def matmul_small(left_mat, right_mat):
    return jnp.sum(left_mat[..., :, :, None, :] * right_mat[..., None, :, :, :], axis=-3)


def matvec_small(matrix, vector):
    return jnp.sum(matrix * vector[..., None, :, :], axis=-2)


def flip_small(matrix):
    return jnp.swapaxes(matrix, -3, -2)


def outer_small(left_vec, right_vec):
    return left_vec[..., :, None, :] * right_vec[..., None, :, :]


def det_three(minor_rows):
    return (minor_rows[0][0] * (minor_rows[1][1] * minor_rows[2][2] - minor_rows[1][2] * minor_rows[2][1])
            - minor_rows[0][1] * (minor_rows[1][0] * minor_rows[2][2] - minor_rows[1][2] * minor_rows[2][0])
            + minor_rows[0][2] * (minor_rows[1][0] * minor_rows[2][1] - minor_rows[1][1] * minor_rows[2][0]))


def invert_small(matrix):
    cofactors = []
    for row_skip in range(4):
        cof_line = []
        for col_skip in range(4):
            minor_rows = [[matrix[..., row_pick, col_pick, :] for col_pick in range(4) if col_pick != col_skip]
                          for row_pick in range(4) if row_pick != row_skip]
            factor = 1.0 if (row_skip + col_skip) % 2 == 0 else -1.0
            cof_line.append(factor * det_three(minor_rows))
        cofactors.append(cof_line)
    determinant = matrix[..., 0, 0, :] * cofactors[0][0]
    for col_pick in range(1, 4):
        determinant = determinant + matrix[..., 0, col_pick, :] * cofactors[0][col_pick]
    adjugate = jnp.stack([jnp.stack([cofactors[col_pick][row_pick] for col_pick in range(4)], axis=-2)
                          for row_pick in range(4)], axis=-3)
    return adjugate / determinant[..., None, None, :]


def rotation_table(angles):
    mode_count = angles.shape[-1]
    identity = jnp.broadcast_to(jnp.eye(4, dtype=angles.dtype)[:, :, None], (4, 4, mode_count))
    result = identity
    planes = ((0, 1), (2, 3), (1, 2), (0, 3))
    for plane_index in range(4):
        first, second = planes[plane_index]
        cos_value = jnp.cos(angles[plane_index])
        sin_value = jnp.sin(angles[plane_index])
        rotate = identity.at[first, first].set(cos_value).at[second, second].set(cos_value)
        rotate = rotate.at[first, second].set(-sin_value).at[second, first].set(sin_value)
        result = matmul_small(rotate, result)
    return result


def step_noise(sensor, noise_var):
    onehot = (sensor[:, None] == jnp.arange(noise_var.shape[0], dtype=jnp.int32)[None, :]).astype(noise_var.dtype)
    return jnp.sum(onehot[:, :, None] * noise_var[None, :, :], axis=1)


def filter_elements(readings, seen_mask, step_var, retain, rotate, field_cov, readout):
    retain_b = retain[:, None, None, :]
    transit = retain_b * rotate
    noise_cov = (1.0 - retain_b * retain_b) * field_cov
    spread = matvec_small(noise_cov, readout)
    innovation = jnp.sum(readout * spread, axis=-2) + step_var
    weight = seen_mask.astype(readings.dtype) / innovation
    kalman_gain = weight[:, None, :] * spread
    identity = jnp.eye(4, dtype=readings.dtype)[:, :, None]
    shrink = identity - outer_small(kalman_gain, readout)
    trans_part = matmul_small(shrink, transit)
    offset = kalman_gain * readings[:, None, :]
    cov_part = noise_cov - weight[:, None, None, :] * outer_small(spread, spread)
    pulled = matvec_small(flip_small(transit), readout)
    info_vec = (weight * readings)[:, None, :] * pulled
    info_mat = weight[:, None, None, :] * outer_small(pulled, pulled)
    return (trans_part, offset, cov_part, info_vec, info_mat)


def apply_filter(incoming, element):
    identity = jnp.eye(4, dtype=element[0].dtype)[:, :, None]
    mixing = invert_small(identity + matmul_small(incoming[1], element[4]))
    carried = matmul_small(element[0], mixing)
    mean_part = matvec_small(carried, incoming[0] + matvec_small(incoming[1], element[3])) + element[1]
    cov_part = matmul_small(matmul_small(carried, incoming[1]), flip_small(element[0])) + element[2]
    return mean_part, cov_part, mixing, carried


def filter_combine(first, second):
    mean_part, cov_part, mixing, carried = apply_filter((first[1], first[2]), second)
    trans_part = matmul_small(carried, first[0])
    pulled = flip_small(matmul_small(mixing, first[0]))
    info_vec = matvec_small(pulled, second[3] - matvec_small(second[4], first[1])) + first[3]
    info_mat = matmul_small(matmul_small(pulled, second[4]), first[0]) + first[4]
    return (trans_part, mean_part, cov_part, info_vec, info_mat)


def smooth_elements(mean_part, cov_part, retain_next, last_step, rotate, field_cov):
    retain_b = retain_next[:, None, None, :]
    transit = retain_b * rotate
    noise_cov = (1.0 - retain_b * retain_b) * field_cov
    predicted = matmul_small(matmul_small(transit, cov_part), flip_small(transit)) + noise_cov
    smoother_gain = matmul_small(matmul_small(cov_part, flip_small(transit)), invert_small(predicted))
    smoother_gain = smoother_gain * (1.0 - last_step)[:, None, None, None]
    offset = mean_part - matvec_small(smoother_gain, matvec_small(transit, mean_part))
    residual_cov = cov_part - matmul_small(matmul_small(smoother_gain, transit), cov_part)
    return (smoother_gain, offset, residual_cov)


def apply_smooth(incoming, element):
    mean_part = matvec_small(element[0], incoming[0]) + element[1]
    cov_part = matmul_small(matmul_small(element[0], incoming[1]), flip_small(element[0])) + element[2]
    return mean_part, cov_part


def smooth_compose(earlier_time, later_time):
    mean_part, cov_part = apply_smooth((later_time[1], later_time[2]), earlier_time)
    return (matmul_small(earlier_time[0], later_time[0]), mean_part, cov_part)


def suffix_scan(elements):
    reversed_elems = tuple(jnp.flip(member, 0) for member in elements)

    def backward(latter, former):
        return smooth_compose(former, latter)

    scanned = lax.associative_scan(backward, reversed_elems)
    return tuple(jnp.flip(member, 0) for member in scanned)


def reference(readings, seen_mask, sensor, time_gaps, noise_var, readout, angles, decay_rates, field_cov):
    real_type = readings.dtype
    rotate = rotation_table(angles)
    step_var = step_noise(sensor, noise_var)
    position = jnp.arange(TIMES, dtype=jnp.int32)
    started = (position > 0).astype(real_type)
    retain = jnp.exp(-decay_rates[None, :] * time_gaps[:, None]) * started[:, None]
    elements = filter_elements(readings, seen_mask, step_var, retain, rotate, field_cov, readout)
    prefix = lax.associative_scan(filter_combine, elements)
    next_gaps = jnp.concatenate([time_gaps[1:], jnp.zeros((1,), real_type)])
    retain_next = jnp.exp(-decay_rates[None, :] * next_gaps[:, None])
    last_step = (position == TIMES - 1).astype(real_type)
    smoothing = smooth_elements(prefix[1], prefix[2], retain_next, last_step, rotate, field_cov)
    suffix = suffix_scan(smoothing)
    log_spread = jnp.log(jnp.sum(readout * matvec_small(suffix[2], readout), axis=-2))
    return suffix[1], log_spread
```

```python
import jax
import jax.numpy as jnp
from jax import lax
from jax.sharding import PartitionSpec as P


def passed_along(x, axis, by):
    count = lax.axis_size(axis)
    pairs = [(i, i + by) for i in range(count) if 0 <= i + by < count]
    return lax.ppermute(x, axis, pairs)


def matmul_small(left_mat, right_mat):
    return jnp.sum(left_mat[..., :, :, None, :] * right_mat[..., None, :, :, :], axis=-3)


def matvec_small(matrix, vector):
    return jnp.sum(matrix * vector[..., None, :, :], axis=-2)


def flip_small(matrix):
    return jnp.swapaxes(matrix, -3, -2)


def outer_small(left_vec, right_vec):
    return left_vec[..., :, None, :] * right_vec[..., None, :, :]


def det_three(minor_rows):
    return (
        minor_rows[0][0]
        * (minor_rows[1][1] * minor_rows[2][2] - minor_rows[1][2] * minor_rows[2][1])
        - minor_rows[0][1]
        * (minor_rows[1][0] * minor_rows[2][2] - minor_rows[1][2] * minor_rows[2][0])
        + minor_rows[0][2]
        * (minor_rows[1][0] * minor_rows[2][1] - minor_rows[1][1] * minor_rows[2][0])
    )


def invert_small(matrix):
    cofactors = []
    for row_skip in range(4):
        cof_line = []
        for col_skip in range(4):
            minor_rows = [
                [
                    matrix[..., row_pick, col_pick, :]
                    for col_pick in range(4)
                    if col_pick != col_skip
                ]
                for row_pick in range(4)
                if row_pick != row_skip
            ]
            factor = 1.0 if (row_skip + col_skip) % 2 == 0 else -1.0
            cof_line.append(factor * det_three(minor_rows))
        cofactors.append(cof_line)
    determinant = matrix[..., 0, 0, :] * cofactors[0][0]
    for col_pick in range(1, 4):
        determinant = determinant + matrix[..., 0, col_pick, :] * cofactors[0][col_pick]
    adjugate = jnp.stack(
        [
            jnp.stack([cofactors[col_pick][row_pick] for col_pick in range(4)], axis=-2)
            for row_pick in range(4)
        ],
        axis=-3,
    )
    return adjugate / determinant[..., None, None, :]


def rotation_table(angles):
    mode_count = angles.shape[-1]
    identity = jnp.broadcast_to(jnp.eye(4, dtype=angles.dtype)[:, :, None], (4, 4, mode_count))
    result = identity
    planes = ((0, 1), (2, 3), (1, 2), (0, 3))
    for plane_index in range(4):
        first, second = planes[plane_index]
        cos_value = jnp.cos(angles[plane_index])
        sin_value = jnp.sin(angles[plane_index])
        rotate = identity.at[first, first].set(cos_value).at[second, second].set(cos_value)
        rotate = rotate.at[first, second].set(-sin_value).at[second, first].set(sin_value)
        result = matmul_small(rotate, result)
    return result


def step_noise(sensor, noise_var):
    onehot = (sensor[:, None] == jnp.arange(noise_var.shape[0], dtype=jnp.int32)[None, :]).astype(
        noise_var.dtype
    )
    return jnp.sum(onehot[:, :, None] * noise_var[None, :, :], axis=1)


def filter_elements(readings, seen_mask, step_var, retain, rotate, field_cov, readout):
    retain_b = retain[:, None, None, :]
    transit = retain_b * rotate
    noise_cov = (1.0 - retain_b * retain_b) * field_cov
    spread = matvec_small(noise_cov, readout)
    innovation = jnp.sum(readout * spread, axis=-2) + step_var
    weight = seen_mask.astype(readings.dtype) / innovation
    kalman_gain = weight[:, None, :] * spread
    identity = jnp.eye(4, dtype=readings.dtype)[:, :, None]
    shrink = identity - outer_small(kalman_gain, readout)
    trans_part = matmul_small(shrink, transit)
    offset = kalman_gain * readings[:, None, :]
    cov_part = noise_cov - weight[:, None, None, :] * outer_small(spread, spread)
    pulled = matvec_small(flip_small(transit), readout)
    info_vec = (weight * readings)[:, None, :] * pulled
    info_mat = weight[:, None, None, :] * outer_small(pulled, pulled)
    return (trans_part, offset, cov_part, info_vec, info_mat)


def apply_filter(incoming, element):
    identity = jnp.eye(4, dtype=element[0].dtype)[:, :, None]
    mixing = invert_small(identity + matmul_small(incoming[1], element[4]))
    carried = matmul_small(element[0], mixing)
    mean_part = (
        matvec_small(carried, incoming[0] + matvec_small(incoming[1], element[3])) + element[1]
    )
    cov_part = matmul_small(matmul_small(carried, incoming[1]), flip_small(element[0])) + element[2]
    return (mean_part, cov_part, mixing, carried)


def filter_combine(first, second):
    mean_part, cov_part, mixing, carried = apply_filter((first[1], first[2]), second)
    trans_part = matmul_small(carried, first[0])
    pulled = flip_small(matmul_small(mixing, first[0]))
    info_vec = matvec_small(pulled, second[3] - matvec_small(second[4], first[1])) + first[3]
    info_mat = matmul_small(matmul_small(pulled, second[4]), first[0]) + first[4]
    return (trans_part, mean_part, cov_part, info_vec, info_mat)


def smooth_elements(mean_part, cov_part, retain_next, last_step, rotate, field_cov):
    retain_b = retain_next[:, None, None, :]
    transit = retain_b * rotate
    noise_cov = (1.0 - retain_b * retain_b) * field_cov
    predicted = matmul_small(matmul_small(transit, cov_part), flip_small(transit)) + noise_cov
    smoother_gain = matmul_small(
        matmul_small(cov_part, flip_small(transit)), invert_small(predicted)
    )
    smoother_gain = smoother_gain * (1.0 - last_step)[:, None, None, None]
    offset = mean_part - matvec_small(smoother_gain, matvec_small(transit, mean_part))
    residual_cov = cov_part - matmul_small(matmul_small(smoother_gain, transit), cov_part)
    return (smoother_gain, offset, residual_cov)


def apply_smooth(incoming, element):
    mean_part = matvec_small(element[0], incoming[0]) + element[1]
    cov_part = (
        matmul_small(matmul_small(element[0], incoming[1]), flip_small(element[0])) + element[2]
    )
    return (mean_part, cov_part)


def smooth_compose(earlier_time, later_time):
    mean_part, cov_part = apply_smooth((later_time[1], later_time[2]), earlier_time)
    return (matmul_small(earlier_time[0], later_time[0]), mean_part, cov_part)


def suffix_scan(elements):
    reversed_elems = tuple((jnp.flip(member, 0) for member in elements))

    def backward(latter, former):
        return smooth_compose(former, latter)

    scanned = lax.associative_scan(backward, reversed_elems)
    return tuple((jnp.flip(member, 0) for member in scanned))


def pack_rows(members):
    mode_count = members[0].shape[-1]
    return jnp.concatenate([member.reshape(-1, mode_count) for member in members], axis=0)


def unpack_rows(packed, shapes):
    lead = packed.shape[:-2]
    mode_count = packed.shape[-1]
    members = []
    offset = 0
    for shape in shapes:
        size = 1
        for dim in shape:
            size *= dim
        members.append(packed[..., offset:offset + size, :].reshape(lead + tuple(shape) + (mode_count,)))
        offset += size
    return tuple(members)


def identity_like(member_shapes, count, mode_count, real_type, eye_slots):
    members = []
    for slot, shape in enumerate(member_shapes):
        if slot in eye_slots:
            eye = jnp.eye(4, dtype=real_type)[None, :, :, None]
            members.append(jnp.broadcast_to(eye, (count,) + tuple(shape) + (mode_count,)))
        else:
            members.append(jnp.zeros((count,) + tuple(shape) + (mode_count,), real_type))
    return tuple(members)


FILTER_SHAPES = ((4, 4), (4,), (4, 4), (4,), (4, 4))
SMOOTH_SHAPES = ((4, 4), (4,), (4, 4))


def device_prefix(gathered, real_type):
    count = gathered[0].shape[0]
    mode_count = gathered[0].shape[-1]
    shift = 1
    while shift < count:
        pad = identity_like(FILTER_SHAPES, shift, mode_count, real_type, (0,))
        earlier = tuple(jnp.concatenate([p, g[:-shift]], axis=0) for p, g in zip(pad, gathered))
        gathered = filter_combine(earlier, gathered)
        shift *= 2
    return gathered


def device_suffix(gathered, real_type):
    count = gathered[0].shape[0]
    mode_count = gathered[0].shape[-1]
    shift = 1
    while shift < count:
        pad = identity_like(SMOOTH_SHAPES, shift, mode_count, real_type, (0,))
        later = tuple(jnp.concatenate([g[shift:], p], axis=0) for p, g in zip(pad, gathered))
        gathered = smooth_compose(gathered, later)
        shift *= 2
    return gathered


def local(
    readings, seen_mask, sensor, time_gaps, noise_var, readout, angles, decay_rates, field_cov
):
    real_type = readings.dtype
    steps_here = readings.shape[0]
    mode_count = readings.shape[1]
    device_count = lax.axis_size("tm")
    device_place = lax.axis_index("tm")
    start_step = device_place * steps_here
    total_steps = device_count * steps_here
    position = start_step + jnp.arange(steps_here, dtype=jnp.int32)
    local_gaps = lax.dynamic_slice_in_dim(time_gaps, start_step, steps_here)
    padded_gaps = jnp.concatenate([time_gaps, jnp.zeros((1,), real_type)])
    next_gaps = lax.dynamic_slice_in_dim(padded_gaps, start_step + 1, steps_here)
    rotate = rotation_table(angles)
    step_var = step_noise(sensor, noise_var)
    started = (position > 0).astype(real_type)
    retain = jnp.exp(-decay_rates[None, :] * local_gaps[:, None]) * started[:, None]
    elements = filter_elements(readings, seen_mask, step_var, retain, rotate, field_cov, readout)
    prefix = lax.associative_scan(filter_combine, elements)
    summary = pack_rows(tuple((member[-1] for member in prefix)))
    gathered = unpack_rows(lax.all_gather(summary, "tm"), FILTER_SHAPES)
    scanned = device_prefix(gathered, real_type)
    before = jnp.maximum(device_place - 1, 0)
    has_before = (device_place > 0).astype(real_type)
    enter_mean = lax.dynamic_index_in_dim(scanned[1], before, keepdims=False) * has_before
    enter_cov = lax.dynamic_index_in_dim(scanned[2], before, keepdims=False) * has_before
    filtered = apply_filter((enter_mean, enter_cov), prefix)
    retain_next = jnp.exp(-decay_rates[None, :] * next_gaps[:, None])
    last_step = (position == total_steps - 1).astype(real_type)
    smoothing = smooth_elements(filtered[0], filtered[1], retain_next, last_step, rotate, field_cov)
    suffix = suffix_scan(smoothing)
    head = pack_rows(tuple((member[0] for member in suffix)))
    gathered_back = unpack_rows(lax.all_gather(head, "tm"), SMOOTH_SHAPES)
    scanned_back = device_suffix(gathered_back, real_type)
    after = jnp.minimum(device_place + 1, device_count - 1)
    has_after = (device_place < device_count - 1).astype(real_type)
    leave_mean = lax.dynamic_index_in_dim(scanned_back[1], after, keepdims=False) * has_after
    leave_cov = lax.dynamic_index_in_dim(scanned_back[2], after, keepdims=False) * has_after
    smoothed = apply_smooth((leave_mean, leave_cov), suffix)
    log_spread = jnp.log(jnp.sum(readout * matvec_small(smoothed[1], readout), axis=-2))
    return (smoothed[0], log_spread)


def solution(mesh):
    return jax.shard_map(
        local,
        mesh=mesh,
        in_specs=(
            P("tm", "ens"),
            P("tm", None),
            P("tm"),
            P(),
            P(None, "ens"),
            P(None, "ens"),
            P(None, "ens"),
            P("ens"),
            P(None, None, "ens"),
        ),
        out_specs=(P("tm", None, "ens"), P("tm", "ens")),
        check_vma=False,
    )
```

```python
import jax
import jax.numpy as jnp
from jax import lax
from jax.experimental import pallas as pl
from jax.experimental.pallas import tpu as pltpu
from jax.sharding import PartitionSpec as P

INTERPRET = False
FILTER_SIZES = (16, 4, 16, 4, 16)
SMOOTH_SIZES = (16, 4, 16)


def eye4(one, zero):
    return [[one if row == col else zero for col in range(4)] for row in range(4)]


def mm(left, right):
    return [
        [
            left[row][0] * right[0][col]
            + left[row][1] * right[1][col]
            + left[row][2] * right[2][col]
            + left[row][3] * right[3][col]
            for col in range(4)
        ]
        for row in range(4)
    ]


def mv(matrix, vector):
    return [
        matrix[row][0] * vector[0]
        + matrix[row][1] * vector[1]
        + matrix[row][2] * vector[2]
        + matrix[row][3] * vector[3]
        for row in range(4)
    ]


def tr(matrix):
    return [[matrix[col][row] for col in range(4)] for row in range(4)]


def madd(left, right):
    return [[left[row][col] + right[row][col] for col in range(4)] for row in range(4)]


def vadd(left, right):
    return [left[row] + right[row] for row in range(4)]


def det3(rows):
    return (
        rows[0][0] * (rows[1][1] * rows[2][2] - rows[1][2] * rows[2][1])
        - rows[0][1] * (rows[1][0] * rows[2][2] - rows[1][2] * rows[2][0])
        + rows[0][2] * (rows[1][0] * rows[2][1] - rows[1][1] * rows[2][0])
    )


def inv4(matrix):
    cof = []
    for row_skip in range(4):
        line = []
        for col_skip in range(4):
            minor = [
                [matrix[r][c] for c in range(4) if c != col_skip] for r in range(4) if r != row_skip
            ]
            value = det3(minor)
            line.append(value if (row_skip + col_skip) % 2 == 0 else -value)
        cof.append(line)
    det = matrix[0][0] * cof[0][0]
    for col in range(1, 4):
        det = det + matrix[0][col] * cof[0][col]
    scale = 1.0 / det
    return [[cof[col][row] * scale for col in range(4)] for row in range(4)]


def to_mat(flat):
    return [[flat[4 * row + col] for col in range(4)] for row in range(4)]


def from_mat(matrix):
    return [matrix[row][col] for row in range(4) for col in range(4)]


def split_flat(flat, sizes):
    parts = []
    offset = 0
    for size in sizes:
        piece = flat[offset:offset + size]
        parts.append(to_mat(piece) if size == 16 else list(piece))
        offset += size
    return parts


def join_flat(parts):
    flat = []
    for part in parts:
        flat.extend(from_mat(part) if isinstance(part[0], list) else part)
    return flat


def filter_combine(first, second):
    trans_i, mean_i, cov_i, vec_i, mat_i = first
    trans_j, mean_j, cov_j, vec_j, mat_j = second
    one = jnp.ones_like(cov_i[0][0])
    zero = jnp.zeros_like(cov_i[0][0])
    mixing = inv4(madd(eye4(one, zero), mm(cov_i, mat_j)))
    carried = mm(trans_j, mixing)
    mean_part = vadd(mv(carried, vadd(mean_i, mv(cov_i, vec_j))), mean_j)
    cov_part = madd(mm(mm(carried, cov_i), tr(trans_j)), cov_j)
    trans_part = mm(carried, trans_i)
    pulled = tr(mm(mixing, trans_i))
    resid = [vec_j[row] - value for row, value in enumerate(mv(mat_j, mean_i))]
    vec_part = vadd(mv(pulled, resid), vec_i)
    mat_part = madd(mm(mm(pulled, mat_j), trans_i), mat_i)
    return [trans_part, mean_part, cov_part, vec_part, mat_part]


def apply_filter(mean_in, cov_in, element):
    trans_j, mean_j, cov_j, vec_j, mat_j = element
    one = jnp.ones_like(cov_j[0][0])
    zero = jnp.zeros_like(cov_j[0][0])
    mixing = inv4(madd(eye4(one, zero), mm(cov_in, mat_j)))
    carried = mm(trans_j, mixing)
    mean_part = vadd(mv(carried, vadd(mean_in, mv(cov_in, vec_j))), mean_j)
    cov_part = madd(mm(mm(carried, cov_in), tr(trans_j)), cov_j)
    return mean_part, cov_part


def smooth_compose(earlier, later):
    gain_e, mean_e, cov_e = earlier
    gain_l, mean_l, cov_l = later
    mean_part = vadd(mv(gain_e, mean_l), mean_e)
    cov_part = madd(mm(mm(gain_e, cov_l), tr(gain_e)), cov_e)
    return [mm(gain_e, gain_l), mean_part, cov_part]


def apply_smooth(mean_in, cov_in, element):
    gain, mean_e, cov_e = element
    mean_part = vadd(mv(gain, mean_in), mean_e)
    cov_part = madd(mm(mm(gain, cov_in), tr(gain)), cov_e)
    return mean_part, cov_part


def identity_flat(sizes, like):
    one = jnp.ones_like(like)
    zero = jnp.zeros_like(like)
    flat = []
    for slot, size in enumerate(sizes):
        if slot == 0:
            flat.extend(from_mat(eye4(one, zero)))
        else:
            flat.extend([zero] * size)
    return flat


def shift_rows(flat, ident, shift, forward):
    count = flat[0].shape[0]
    row = lax.broadcasted_iota(jnp.int32, flat[0].shape, 0)
    out = []
    for value, pad in zip(flat, ident):
        if forward:
            moved = pltpu.roll(value, shift, 0)
            out.append(jnp.where(row >= shift, moved, pad))
        else:
            moved = pltpu.roll(value, count - shift, 0)
            out.append(jnp.where(row < count - shift, moved, pad))
    return out


def prefix_rows(flat):
    count = flat[0].shape[0]
    ident = identity_flat(FILTER_SIZES, flat[0])
    shift = 1
    while shift < count:
        earlier = shift_rows(flat, ident, shift, True)
        flat = join_flat(
            filter_combine(split_flat(earlier, FILTER_SIZES), split_flat(flat, FILTER_SIZES))
        )
        shift *= 2
    return flat


def suffix_rows(flat):
    count = flat[0].shape[0]
    ident = identity_flat(SMOOTH_SIZES, flat[0])
    shift = 1
    while shift < count:
        later = shift_rows(flat, ident, shift, False)
        flat = join_flat(
            smooth_compose(split_flat(flat, SMOOTH_SIZES), split_flat(later, SMOOTH_SIZES))
        )
        shift *= 2
    return flat


def filter_kernel(obs_ref, seen_ref, var_ref, keep_ref, rot_ref, fcov_ref, read_ref, out_ref):
    obs = obs_ref[...]
    seen = seen_ref[...]
    keep = keep_ref[...]
    rot = [[rot_ref[4 * r + c] for c in range(4)] for r in range(4)]
    fcov = [[fcov_ref[4 * r + c] for c in range(4)] for r in range(4)]
    read = [read_ref[r] for r in range(4)]
    trans = [[keep * rot[r][c] for c in range(4)] for r in range(4)]
    fade = 1.0 - keep * keep
    noise = [[fade * fcov[r][c] for c in range(4)] for r in range(4)]
    spread = mv(noise, read)
    innov = (
        read[0] * spread[0] + read[1] * spread[1] + read[2] * spread[2] + read[3] * spread[3]
    ) + var_ref[...]
    weight = seen / innov
    gain = [weight * spread[r] for r in range(4)]
    shrink = [
        [(1.0 if r == c else 0.0) - gain[r] * read[c] for c in range(4)] for r in range(4)
    ]
    trans_part = mm(shrink, trans)
    offset = [gain[r] * obs for r in range(4)]
    cov_part = [[noise[r][c] - weight * spread[r] * spread[c] for c in range(4)] for r in range(4)]
    pulled = mv(tr(trans), read)
    wy = weight * obs
    vec_part = [wy * pulled[r] for r in range(4)]
    mat_part = [[weight * pulled[r] * pulled[c] for c in range(4)] for r in range(4)]
    flat = join_flat([trans_part, offset, cov_part, vec_part, mat_part])
    flat = prefix_rows(flat)
    for index, value in enumerate(flat):
        out_ref[index] = value


def middle_kernel(recv_ref, pre_ref, keep_ref, last_ref, rot_ref, fcov_ref, out_ref):
    devices = recv_ref.shape[1]
    recv = prefix_rows([recv_ref[index] for index in range(56)])
    enter = split_flat([value[devices - 1:devices] for value in recv], FILTER_SIZES)
    element = split_flat([pre_ref[index] for index in range(56)], FILTER_SIZES)
    mean_f, cov_f = apply_filter(enter[1], enter[2], element)
    keep = keep_ref[...]
    rot = [[rot_ref[4 * r + c] for c in range(4)] for r in range(4)]
    fcov = [[fcov_ref[4 * r + c] for c in range(4)] for r in range(4)]
    trans = [[keep * rot[r][c] for c in range(4)] for r in range(4)]
    fade = 1.0 - keep * keep
    noise = [[fade * fcov[r][c] for c in range(4)] for r in range(4)]
    trans_t = tr(trans)
    predicted = madd(mm(mm(trans, cov_f), trans_t), noise)
    live = 1.0 - last_ref[...]
    gain = mm(mm(cov_f, trans_t), inv4(predicted))
    gain = [[gain[r][c] * live for c in range(4)] for r in range(4)]
    pushed = mv(gain, mv(trans, mean_f))
    offset = [mean_f[r] - pushed[r] for r in range(4)]
    taken = mm(mm(gain, trans), cov_f)
    resid = [[cov_f[r][c] - taken[r][c] for c in range(4)] for r in range(4)]
    flat = suffix_rows(join_flat([gain, offset, resid]))
    for index, value in enumerate(flat):
        out_ref[index] = value


def final_kernel(recv_ref, suf_ref, read_ref, mean_ref, spread_ref):
    recv = suffix_rows([recv_ref[index] for index in range(36)])
    leave = split_flat([value[0:1] for value in recv], SMOOTH_SIZES)
    element = split_flat([suf_ref[index] for index in range(36)], SMOOTH_SIZES)
    mean_s, cov_s = apply_smooth(leave[1], leave[2], element)
    read = [read_ref[r] for r in range(4)]
    for r in range(4):
        mean_ref[r] = mean_s[r]
    proj = mv(cov_s, read)
    total = read[0] * proj[0] + read[1] * proj[1] + read[2] * proj[2] + read[3] * proj[3]
    spread_ref[...] = jnp.log(total)


def run_kernel(kernel, out_shapes, *args):
    return pl.pallas_call(kernel, out_shape=out_shapes, interpret=INTERPRET)(*args)


def rotation_flat(angles):
    mode_count = angles.shape[-1]
    one = jnp.ones((mode_count,), angles.dtype)
    zero = jnp.zeros((mode_count,), angles.dtype)
    result = eye4(one, zero)
    planes = ((0, 1), (2, 3), (1, 2), (0, 3))
    for plane_index in range(4):
        first, second = planes[plane_index]
        cos_value = jnp.cos(angles[plane_index])
        sin_value = jnp.sin(angles[plane_index])
        rotate = eye4(one, zero)
        rotate[first][first] = cos_value
        rotate[second][second] = cos_value
        rotate[first][second] = -sin_value
        rotate[second][first] = sin_value
        result = mm(rotate, result)
    return jnp.stack(from_mat(result), axis=0)[:, None, :]


def exchange(summary, forward):
    count = lax.axis_size("tm")
    rows = [jnp.zeros_like(summary)] if forward else []
    shifts = range(count - 1, 0, -1) if forward else range(1, count)
    for shift in shifts:
        if forward:
            pairs = [(i, i + shift) for i in range(count - shift)]
        else:
            pairs = [(i, i - shift) for i in range(shift, count)]
        rows.append(lax.ppermute(summary, "tm", pairs))
    if not forward:
        rows.append(jnp.zeros_like(summary))
    return jnp.stack(rows, axis=1)


def local(
    readings, seen_mask, sensor, time_gaps, noise_var, readout, angles, decay_rates, field_cov
):
    real_type = readings.dtype
    steps_here = readings.shape[0]
    mode_count = readings.shape[1]
    device_count = lax.axis_size("tm")
    device_place = lax.axis_index("tm")
    start_step = device_place * steps_here
    total_steps = device_count * steps_here
    position = start_step + jnp.arange(steps_here, dtype=jnp.int32)
    local_gaps = lax.dynamic_slice_in_dim(time_gaps, start_step, steps_here)
    padded_gaps = jnp.concatenate([time_gaps, jnp.zeros((1,), real_type)])
    next_gaps = lax.dynamic_slice_in_dim(padded_gaps, start_step + 1, steps_here)
    rot = rotation_flat(angles)
    fcov = field_cov.reshape(16, 1, mode_count)
    read = readout[:, None, :]
    onehot = (sensor[:, None] == jnp.arange(noise_var.shape[0], dtype=jnp.int32)[None, :])
    step_var = jnp.sum(onehot.astype(real_type)[:, :, None] * noise_var[None, :, :], axis=1)
    started = (position > 0).astype(real_type)
    retain = jnp.exp(-decay_rates[None, :] * local_gaps[:, None]) * started[:, None]
    retain_next = jnp.exp(-decay_rates[None, :] * next_gaps[:, None])
    last_step = jnp.broadcast_to(
        (position == total_steps - 1).astype(real_type)[:, None], (steps_here, mode_count)
    )
    seen = seen_mask.astype(real_type)
    prefix = run_kernel(
        filter_kernel,
        jax.ShapeDtypeStruct((56, steps_here, mode_count), real_type),
        readings, seen, step_var, retain, rot, fcov, read,
    )
    recv = exchange(prefix[:, steps_here - 1, :], True)
    suffix = run_kernel(
        middle_kernel,
        jax.ShapeDtypeStruct((36, steps_here, mode_count), real_type),
        recv, prefix, retain_next, last_step, rot, fcov,
    )
    recv_back = exchange(suffix[:, 0, :], False)
    mean_out, log_spread = run_kernel(
        final_kernel,
        (
            jax.ShapeDtypeStruct((4, steps_here, mode_count), real_type),
            jax.ShapeDtypeStruct((steps_here, mode_count), real_type),
        ),
        recv_back, suffix, read,
    )
    return (jnp.transpose(mean_out, (1, 0, 2)), log_spread)


def solution(mesh):
    return jax.shard_map(
        local,
        mesh=mesh,
        in_specs=(
            P("tm", "ens"),
            P("tm", None),
            P("tm"),
            P(),
            P(None, "ens"),
            P(None, "ens"),
            P(None, "ens"),
            P("ens"),
            P(None, None, "ens"),
        ),
        out_specs=(P("tm", None, "ens"), P("tm", "ens")),
        check_vma=False,
    )
```

```python
import jax
import jax.numpy as jnp
from jax import lax
from jax.experimental import pallas as pl
from jax.experimental.pallas import tpu as pltpu
from jax.sharding import PartitionSpec as P

INTERPRET = False
FILTER_SIZES = (16, 4, 16, 4, 16)
SMOOTH_SIZES = (16, 4, 16)


def eye4(one, zero):
    return [[one if row == col else zero for col in range(4)] for row in range(4)]


def mm(left, right):
    return [
        [
            left[row][0] * right[0][col]
            + left[row][1] * right[1][col]
            + left[row][2] * right[2][col]
            + left[row][3] * right[3][col]
            for col in range(4)
        ]
        for row in range(4)
    ]


def mv(matrix, vector):
    return [
        matrix[row][0] * vector[0]
        + matrix[row][1] * vector[1]
        + matrix[row][2] * vector[2]
        + matrix[row][3] * vector[3]
        for row in range(4)
    ]


def tr(matrix):
    return [[matrix[col][row] for col in range(4)] for row in range(4)]


def madd(left, right):
    return [[left[row][col] + right[row][col] for col in range(4)] for row in range(4)]


def vadd(left, right):
    return [left[row] + right[row] for row in range(4)]


def det3(rows):
    return (
        rows[0][0] * (rows[1][1] * rows[2][2] - rows[1][2] * rows[2][1])
        - rows[0][1] * (rows[1][0] * rows[2][2] - rows[1][2] * rows[2][0])
        + rows[0][2] * (rows[1][0] * rows[2][1] - rows[1][1] * rows[2][0])
    )


def inv4(matrix):
    cof = []
    for row_skip in range(4):
        line = []
        for col_skip in range(4):
            minor = [
                [matrix[r][c] for c in range(4) if c != col_skip] for r in range(4) if r != row_skip
            ]
            value = det3(minor)
            line.append(value if (row_skip + col_skip) % 2 == 0 else -value)
        cof.append(line)
    det = matrix[0][0] * cof[0][0]
    for col in range(1, 4):
        det = det + matrix[0][col] * cof[0][col]
    scale = 1.0 / det
    return [[cof[col][row] * scale for col in range(4)] for row in range(4)]


def to_mat(flat):
    return [[flat[4 * row + col] for col in range(4)] for row in range(4)]


def from_mat(matrix):
    return [matrix[row][col] for row in range(4) for col in range(4)]


def split_flat(flat, sizes):
    parts = []
    offset = 0
    for size in sizes:
        piece = flat[offset:offset + size]
        parts.append(to_mat(piece) if size == 16 else list(piece))
        offset += size
    return parts


def join_flat(parts):
    flat = []
    for part in parts:
        flat.extend(from_mat(part) if isinstance(part[0], list) else part)
    return flat


def filter_combine(first, second):
    trans_i, mean_i, cov_i, vec_i, mat_i = first
    trans_j, mean_j, cov_j, vec_j, mat_j = second
    one = jnp.ones_like(cov_i[0][0])
    zero = jnp.zeros_like(cov_i[0][0])
    mixing = inv4(madd(eye4(one, zero), mm(cov_i, mat_j)))
    carried = mm(trans_j, mixing)
    mean_part = vadd(mv(carried, vadd(mean_i, mv(cov_i, vec_j))), mean_j)
    cov_part = madd(mm(mm(carried, cov_i), tr(trans_j)), cov_j)
    trans_part = mm(carried, trans_i)
    pulled = tr(mm(mixing, trans_i))
    resid = [vec_j[row] - value for row, value in enumerate(mv(mat_j, mean_i))]
    vec_part = vadd(mv(pulled, resid), vec_i)
    mat_part = madd(mm(mm(pulled, mat_j), trans_i), mat_i)
    return [trans_part, mean_part, cov_part, vec_part, mat_part]


def apply_filter(mean_in, cov_in, element):
    trans_j, mean_j, cov_j, vec_j, mat_j = element
    one = jnp.ones_like(cov_j[0][0])
    zero = jnp.zeros_like(cov_j[0][0])
    mixing = inv4(madd(eye4(one, zero), mm(cov_in, mat_j)))
    carried = mm(trans_j, mixing)
    mean_part = vadd(mv(carried, vadd(mean_in, mv(cov_in, vec_j))), mean_j)
    cov_part = madd(mm(mm(carried, cov_in), tr(trans_j)), cov_j)
    return mean_part, cov_part


def smooth_compose(earlier, later):
    gain_e, mean_e, cov_e = earlier
    gain_l, mean_l, cov_l = later
    mean_part = vadd(mv(gain_e, mean_l), mean_e)
    cov_part = madd(mm(mm(gain_e, cov_l), tr(gain_e)), cov_e)
    return [mm(gain_e, gain_l), mean_part, cov_part]


def apply_smooth(mean_in, cov_in, element):
    gain, mean_e, cov_e = element
    mean_part = vadd(mv(gain, mean_in), mean_e)
    cov_part = madd(mm(mm(gain, cov_in), tr(gain)), cov_e)
    return mean_part, cov_part


def identity_flat(sizes, like):
    one = jnp.ones_like(like)
    zero = jnp.zeros_like(like)
    flat = []
    for slot, size in enumerate(sizes):
        if slot == 0:
            flat.extend(from_mat(eye4(one, zero)))
        else:
            flat.extend([zero] * size)
    return flat


def shift_rows(flat, ident, shift, forward):
    count = flat[0].shape[0]
    row = lax.broadcasted_iota(jnp.int32, flat[0].shape, 0)
    out = []
    for value, pad in zip(flat, ident):
        if forward:
            moved = pltpu.roll(value, shift, 0)
            out.append(jnp.where(row >= shift, moved, pad))
        else:
            moved = pltpu.roll(value, count - shift, 0)
            out.append(jnp.where(row < count - shift, moved, pad))
    return out


def prefix_rows(flat):
    count = flat[0].shape[0]
    ident = identity_flat(FILTER_SIZES, flat[0])
    shift = 1
    while shift < count:
        earlier = shift_rows(flat, ident, shift, True)
        flat = join_flat(
            filter_combine(split_flat(earlier, FILTER_SIZES), split_flat(flat, FILTER_SIZES))
        )
        shift *= 2
    return flat


def suffix_rows(flat):
    count = flat[0].shape[0]
    ident = identity_flat(SMOOTH_SIZES, flat[0])
    shift = 1
    while shift < count:
        later = shift_rows(flat, ident, shift, False)
        flat = join_flat(
            smooth_compose(split_flat(flat, SMOOTH_SIZES), split_flat(later, SMOOTH_SIZES))
        )
        shift *= 2
    return flat


def row_mat(ref):
    return [[ref[4 * r + c:4 * r + c + 1, :] for c in range(4)] for r in range(4)]


def cube_mat(ref):
    return [[ref[r, c:c + 1, :] for c in range(4)] for r in range(4)]


def filter_kernel(obs_ref, seen_ref, var_ref, keep_ref, rot_ref, fcov_ref, read_ref, out_ref, sum_ref):
    obs = obs_ref[...]
    seen = seen_ref[...].astype(obs.dtype)
    keep = keep_ref[...]
    rot = row_mat(rot_ref)
    fcov = cube_mat(fcov_ref)
    read = [read_ref[r:r + 1, :] for r in range(4)]
    trans = [[keep * rot[r][c] for c in range(4)] for r in range(4)]
    fade = 1.0 - keep * keep
    noise = [[fade * fcov[r][c] for c in range(4)] for r in range(4)]
    spread = mv(noise, read)
    innov = (
        read[0] * spread[0] + read[1] * spread[1] + read[2] * spread[2] + read[3] * spread[3]
    ) + var_ref[...]
    weight = seen / innov
    gain = [weight * spread[r] for r in range(4)]
    shrink = [
        [(1.0 if r == c else 0.0) - gain[r] * read[c] for c in range(4)] for r in range(4)
    ]
    trans_part = mm(shrink, trans)
    offset = [gain[r] * obs for r in range(4)]
    cov_part = [[noise[r][c] - weight * spread[r] * spread[c] for c in range(4)] for r in range(4)]
    pulled = mv(tr(trans), read)
    wy = weight * obs
    vec_part = [wy * pulled[r] for r in range(4)]
    mat_part = [[weight * pulled[r] * pulled[c] for c in range(4)] for r in range(4)]
    flat = join_flat([trans_part, offset, cov_part, vec_part, mat_part])
    flat = prefix_rows(flat)
    steps = flat[0].shape[0]
    for index, value in enumerate(flat):
        out_ref[index] = value
        sum_ref[index:index + 1, :] = value[steps - 1:steps]


def fold_filter(place, recv_refs):
    count = len(recv_refs) + 1
    mean = None
    cov = None
    for shift in range(count - 1, 0, -1):
        ref = recv_refs[shift - 1]
        element = split_flat([ref[index:index + 1, :] for index in range(56)], FILTER_SIZES)
        if mean is None:
            zero = jnp.zeros_like(element[1][0])
            mean = [zero] * 4
            cov = [[zero] * 4 for _ in range(4)]
        new_mean, new_cov = apply_filter(mean, cov, element)
        take = place >= shift
        mean = [jnp.where(take, a, b) for a, b in zip(new_mean, mean)]
        cov = [[jnp.where(take, a, b) for a, b in zip(ra, rb)] for ra, rb in zip(new_cov, cov)]
    return mean, cov


def fold_smooth(place, recv_refs):
    count = len(recv_refs) + 1
    mean = None
    cov = None
    for shift in range(count - 1, 0, -1):
        ref = recv_refs[shift - 1]
        element = split_flat([ref[index:index + 1, :] for index in range(36)], SMOOTH_SIZES)
        if mean is None:
            zero = jnp.zeros_like(element[1][0])
            mean = [zero] * 4
            cov = [[zero] * 4 for _ in range(4)]
        new_mean, new_cov = apply_smooth(mean, cov, element)
        take = place + shift <= count - 1
        mean = [jnp.where(take, a, b) for a, b in zip(new_mean, mean)]
        cov = [[jnp.where(take, a, b) for a, b in zip(ra, rb)] for ra, rb in zip(new_cov, cov)]
    return mean, cov


def middle_kernel(place_ref, pre_ref, keep_ref, last_ref, rot_ref, fcov_ref, *rest):
    recv_refs = rest[:-2]
    out_ref, head_ref = rest[-2:]
    place = place_ref[0]
    enter_mean, enter_cov = fold_filter(place, recv_refs)
    element = split_flat([pre_ref[index] for index in range(56)], FILTER_SIZES)
    mean_f, cov_f = apply_filter(enter_mean, enter_cov, element)
    keep = keep_ref[...]
    rot = row_mat(rot_ref)
    fcov = cube_mat(fcov_ref)
    trans = [[keep * rot[r][c] for c in range(4)] for r in range(4)]
    fade = 1.0 - keep * keep
    noise = [[fade * fcov[r][c] for c in range(4)] for r in range(4)]
    trans_t = tr(trans)
    predicted = madd(mm(mm(trans, cov_f), trans_t), noise)
    live = 1.0 - last_ref[...]
    gain = mm(mm(cov_f, trans_t), inv4(predicted))
    gain = [[gain[r][c] * live for c in range(4)] for r in range(4)]
    pushed = mv(gain, mv(trans, mean_f))
    offset = [mean_f[r] - pushed[r] for r in range(4)]
    taken = mm(mm(gain, trans), cov_f)
    resid = [[cov_f[r][c] - taken[r][c] for c in range(4)] for r in range(4)]
    flat = suffix_rows(join_flat([gain, offset, resid]))
    for index, value in enumerate(flat):
        out_ref[index] = value
        head_ref[index:index + 1, :] = value[0:1]


def final_kernel(place_ref, suf_ref, read_ref, *rest):
    recv_refs = rest[:-2]
    mean_ref, spread_ref = rest[-2:]
    place = place_ref[0]
    leave_mean, leave_cov = fold_smooth(place, recv_refs)
    element = split_flat([suf_ref[index] for index in range(36)], SMOOTH_SIZES)
    mean_s, cov_s = apply_smooth(leave_mean, leave_cov, element)
    read = [read_ref[r:r + 1, :] for r in range(4)]
    for r in range(4):
        mean_ref[:, r, :] = mean_s[r]
    proj = mv(cov_s, read)
    total = read[0] * proj[0] + read[1] * proj[1] + read[2] * proj[2] + read[3] * proj[3]
    spread_ref[...] = jnp.log(total)


def run_kernel(kernel, out_shapes, smem_count, *args):
    specs = [pl.BlockSpec(memory_space=pltpu.SMEM)] * smem_count
    specs += [pl.BlockSpec(memory_space=pltpu.VMEM)] * (len(args) - smem_count)
    return pl.pallas_call(kernel, out_shape=out_shapes, in_specs=specs, interpret=INTERPRET)(*args)


def rotation_flat(angles):
    mode_count = angles.shape[-1]
    one = jnp.ones((mode_count,), angles.dtype)
    zero = jnp.zeros((mode_count,), angles.dtype)
    result = eye4(one, zero)
    planes = ((0, 1), (2, 3), (1, 2), (0, 3))
    for plane_index in range(4):
        first, second = planes[plane_index]
        cos_value = jnp.cos(angles[plane_index])
        sin_value = jnp.sin(angles[plane_index])
        rotate = eye4(one, zero)
        rotate[first][first] = cos_value
        rotate[second][second] = cos_value
        rotate[first][second] = -sin_value
        rotate[second][first] = sin_value
        result = mm(rotate, result)
    return jnp.stack(from_mat(result), axis=0)


def exchange(summary, forward):
    count = lax.axis_size("tm")
    received = []
    for shift in range(1, count):
        if forward:
            pairs = [(i, (i + shift) % count) for i in range(count)]
        else:
            pairs = [(i, (i - shift) % count) for i in range(count)]
        received.append(lax.ppermute(summary, "tm", pairs))
    return received


def local(
    readings, seen_mask, sensor, time_gaps, noise_var, readout, angles, decay_rates, field_cov
):
    real_type = readings.dtype
    steps_here = readings.shape[0]
    mode_count = readings.shape[1]
    device_count = lax.axis_size("tm")
    device_place = lax.axis_index("tm")
    start_step = device_place * steps_here
    total_steps = device_count * steps_here
    position = start_step + jnp.arange(steps_here, dtype=jnp.int32)
    local_gaps = lax.dynamic_slice_in_dim(time_gaps, start_step, steps_here)
    padded_gaps = jnp.concatenate([time_gaps, jnp.zeros((1,), real_type)])
    next_gaps = lax.dynamic_slice_in_dim(padded_gaps, start_step + 1, steps_here)
    rot = rotation_flat(angles)
    onehot = (sensor[:, None] == jnp.arange(noise_var.shape[0], dtype=jnp.int32)[None, :])
    step_var = jnp.sum(onehot.astype(real_type)[:, :, None] * noise_var[None, :, :], axis=1)
    started = (position > 0).astype(real_type)
    retain = jnp.exp(-decay_rates[None, :] * local_gaps[:, None]) * started[:, None]
    retain_next = jnp.exp(-decay_rates[None, :] * next_gaps[:, None])
    last_step = jnp.broadcast_to(
        (position == total_steps - 1).astype(real_type)[:, None], (steps_here, mode_count)
    )
    place = jnp.reshape(device_place, (1,)).astype(jnp.int32)
    prefix, summary = run_kernel(
        filter_kernel,
        (
            jax.ShapeDtypeStruct((56, steps_here, mode_count), real_type),
            jax.ShapeDtypeStruct((56, mode_count), real_type),
        ),
        0,
        readings, seen_mask, step_var, retain, rot, field_cov, readout,
    )
    received = exchange(summary, True)
    suffix, head = run_kernel(
        middle_kernel,
        (
            jax.ShapeDtypeStruct((36, steps_here, mode_count), real_type),
            jax.ShapeDtypeStruct((36, mode_count), real_type),
        ),
        1,
        place, prefix, retain_next, last_step, rot, field_cov, *received,
    )
    received_back = exchange(head, False)
    mean_out, log_spread = run_kernel(
        final_kernel,
        (
            jax.ShapeDtypeStruct((steps_here, 4, mode_count), real_type),
            jax.ShapeDtypeStruct((steps_here, mode_count), real_type),
        ),
        1,
        place, suffix, readout, *received_back,
    )
    return (mean_out, log_spread)


def solution(mesh):
    return jax.shard_map(
        local,
        mesh=mesh,
        in_specs=(
            P("tm", "ens"),
            P("tm", None),
            P("tm"),
            P(),
            P(None, "ens"),
            P(None, "ens"),
            P(None, "ens"),
            P("ens"),
            P(None, None, "ens"),
        ),
        out_specs=(P("tm", None, "ens"), P("tm", "ens")),
        check_vma=False,
    )
```

```python
import jax
import jax.numpy as jnp
from jax import lax
from jax.experimental import pallas as pl
from jax.experimental.pallas import tpu as pltpu
from jax.sharding import PartitionSpec as P

INTERPRET = False
FILTER_SIZES = (16, 4, 16, 4, 16)
SMOOTH_SIZES = (16, 4, 16)


def eye4(one, zero):
    return [[one if row == col else zero for col in range(4)] for row in range(4)]


def mm(left, right):
    return [
        [
            left[row][0] * right[0][col]
            + left[row][1] * right[1][col]
            + left[row][2] * right[2][col]
            + left[row][3] * right[3][col]
            for col in range(4)
        ]
        for row in range(4)
    ]


def mv(matrix, vector):
    return [
        matrix[row][0] * vector[0]
        + matrix[row][1] * vector[1]
        + matrix[row][2] * vector[2]
        + matrix[row][3] * vector[3]
        for row in range(4)
    ]


def tr(matrix):
    return [[matrix[col][row] for col in range(4)] for row in range(4)]


def madd(left, right):
    return [[left[row][col] + right[row][col] for col in range(4)] for row in range(4)]


def vadd(left, right):
    return [left[row] + right[row] for row in range(4)]


def det3(rows):
    return (
        rows[0][0] * (rows[1][1] * rows[2][2] - rows[1][2] * rows[2][1])
        - rows[0][1] * (rows[1][0] * rows[2][2] - rows[1][2] * rows[2][0])
        + rows[0][2] * (rows[1][0] * rows[2][1] - rows[1][1] * rows[2][0])
    )


def inv4(matrix):
    cof = []
    for row_skip in range(4):
        line = []
        for col_skip in range(4):
            minor = [
                [matrix[r][c] for c in range(4) if c != col_skip] for r in range(4) if r != row_skip
            ]
            value = det3(minor)
            line.append(value if (row_skip + col_skip) % 2 == 0 else -value)
        cof.append(line)
    det = matrix[0][0] * cof[0][0]
    for col in range(1, 4):
        det = det + matrix[0][col] * cof[0][col]
    scale = 1.0 / det
    return [[cof[col][row] * scale for col in range(4)] for row in range(4)]


def to_mat(flat):
    return [[flat[4 * row + col] for col in range(4)] for row in range(4)]


def from_mat(matrix):
    return [matrix[row][col] for row in range(4) for col in range(4)]


def split_flat(flat, sizes):
    parts = []
    offset = 0
    for size in sizes:
        piece = flat[offset:offset + size]
        parts.append(to_mat(piece) if size == 16 else list(piece))
        offset += size
    return parts


def join_flat(parts):
    flat = []
    for part in parts:
        flat.extend(from_mat(part) if isinstance(part[0], list) else part)
    return flat


def filter_combine(first, second):
    trans_i, mean_i, cov_i, vec_i, mat_i = first
    trans_j, mean_j, cov_j, vec_j, mat_j = second
    one = jnp.ones_like(cov_i[0][0])
    zero = jnp.zeros_like(cov_i[0][0])
    mixing = inv4(madd(eye4(one, zero), mm(cov_i, mat_j)))
    carried = mm(trans_j, mixing)
    mean_part = vadd(mv(carried, vadd(mean_i, mv(cov_i, vec_j))), mean_j)
    cov_part = madd(mm(mm(carried, cov_i), tr(trans_j)), cov_j)
    trans_part = mm(carried, trans_i)
    pulled = tr(mm(mixing, trans_i))
    resid = [vec_j[row] - value for row, value in enumerate(mv(mat_j, mean_i))]
    vec_part = vadd(mv(pulled, resid), vec_i)
    mat_part = madd(mm(mm(pulled, mat_j), trans_i), mat_i)
    return [trans_part, mean_part, cov_part, vec_part, mat_part]


def apply_filter(mean_in, cov_in, element):
    trans_j, mean_j, cov_j, vec_j, mat_j = element
    one = jnp.ones_like(cov_j[0][0])
    zero = jnp.zeros_like(cov_j[0][0])
    mixing = inv4(madd(eye4(one, zero), mm(cov_in, mat_j)))
    carried = mm(trans_j, mixing)
    mean_part = vadd(mv(carried, vadd(mean_in, mv(cov_in, vec_j))), mean_j)
    cov_part = madd(mm(mm(carried, cov_in), tr(trans_j)), cov_j)
    return mean_part, cov_part


def smooth_compose(earlier, later):
    gain_e, mean_e, cov_e = earlier
    gain_l, mean_l, cov_l = later
    mean_part = vadd(mv(gain_e, mean_l), mean_e)
    cov_part = madd(mm(mm(gain_e, cov_l), tr(gain_e)), cov_e)
    return [mm(gain_e, gain_l), mean_part, cov_part]


def apply_smooth(mean_in, cov_in, element):
    gain, mean_e, cov_e = element
    mean_part = vadd(mv(gain, mean_in), mean_e)
    cov_part = madd(mm(mm(gain, cov_in), tr(gain)), cov_e)
    return mean_part, cov_part


def identity_flat(sizes, like):
    one = jnp.ones_like(like)
    zero = jnp.zeros_like(like)
    flat = []
    for slot, size in enumerate(sizes):
        if slot == 0:
            flat.extend(from_mat(eye4(one, zero)))
        else:
            flat.extend([zero] * size)
    return flat


def shift_rows(flat, ident, shift, forward):
    count = flat[0].shape[0]
    row = lax.broadcasted_iota(jnp.int32, flat[0].shape, 0)
    out = []
    for value, pad in zip(flat, ident):
        if forward:
            moved = pltpu.roll(value, shift, 0)
            out.append(jnp.where(row >= shift, moved, pad))
        else:
            moved = pltpu.roll(value, count - shift, 0)
            out.append(jnp.where(row < count - shift, moved, pad))
    return out


def prefix_rows(flat):
    count = flat[0].shape[0]
    ident = identity_flat(FILTER_SIZES, flat[0])
    shift = 1
    while shift < count:
        earlier = shift_rows(flat, ident, shift, True)
        flat = join_flat(
            filter_combine(split_flat(earlier, FILTER_SIZES), split_flat(flat, FILTER_SIZES))
        )
        shift *= 2
    return flat


def suffix_rows(flat):
    count = flat[0].shape[0]
    ident = identity_flat(SMOOTH_SIZES, flat[0])
    shift = 1
    while shift < count:
        later = shift_rows(flat, ident, shift, False)
        flat = join_flat(
            smooth_compose(split_flat(flat, SMOOTH_SIZES), split_flat(later, SMOOTH_SIZES))
        )
        shift *= 2
    return flat


def row_mat(ref):
    return [[ref[4 * r + c:4 * r + c + 1, :] for c in range(4)] for r in range(4)]


def cube_mat(ref):
    return [[ref[r, c:c + 1, :] for c in range(4)] for r in range(4)]


def filter_kernel(
    place_ref, gaps_ref, sensor_ref, obs_ref, seen_ref, noise_ref, read_ref, angle_ref, decay_ref,
    fcov_ref, out_ref, sum_ref, rot_ref, next_ref,
):
    steps, modes = obs_ref.shape
    total = gaps_ref.shape[0]
    start = place_ref[0] * steps
    row = lax.broadcasted_iota(jnp.int32, (steps, modes), 0)
    zero = jnp.zeros((steps, modes), jnp.float32)
    gap_here = zero
    gap_next = zero
    step_var = zero
    for k in range(steps):
        here = row == k
        gap_here = jnp.where(here, gaps_ref[start + k], gap_here)
        later = jnp.minimum(start + k + 1, total - 1)
        gap_next = jnp.where(here & (start + k + 1 < total), gaps_ref[later], gap_next)
        step_var = jnp.where(here, noise_ref[pl.ds(sensor_ref[k], 1), :], step_var)
    decay = decay_ref[...]
    keep = jnp.where(row + start > 0, jnp.exp(-decay * gap_here), 0.0)
    next_ref[...] = jnp.exp(-decay * gap_next)
    one = jnp.ones((1, modes), jnp.float32)
    flat_zero = jnp.zeros((1, modes), jnp.float32)
    rot = eye4(one, flat_zero)
    planes = ((0, 1), (2, 3), (1, 2), (0, 3))
    for plane_index in range(4):
        first, second = planes[plane_index]
        angle = angle_ref[plane_index:plane_index + 1, :]
        cos_value = jnp.cos(angle)
        sin_value = jnp.sin(angle)
        rotate = eye4(one, flat_zero)
        rotate[first][first] = cos_value
        rotate[second][second] = cos_value
        rotate[first][second] = -sin_value
        rotate[second][first] = sin_value
        rot = mm(rotate, rot)
    for index, value in enumerate(from_mat(rot)):
        rot_ref[index:index + 1, :] = value
    obs = obs_ref[...]
    seen = seen_ref[...].astype(obs.dtype)
    fcov = cube_mat(fcov_ref)
    read = [read_ref[r:r + 1, :] for r in range(4)]
    trans = [[keep * rot[r][c] for c in range(4)] for r in range(4)]
    fade = 1.0 - keep * keep
    noise = [[fade * fcov[r][c] for c in range(4)] for r in range(4)]
    spread = mv(noise, read)
    innov = (
        read[0] * spread[0] + read[1] * spread[1] + read[2] * spread[2] + read[3] * spread[3]
    ) + step_var
    weight = seen / innov
    gain = [weight * spread[r] for r in range(4)]
    shrink = [
        [(1.0 if r == c else 0.0) - gain[r] * read[c] for c in range(4)] for r in range(4)
    ]
    trans_part = mm(shrink, trans)
    offset = [gain[r] * obs for r in range(4)]
    cov_part = [[noise[r][c] - weight * spread[r] * spread[c] for c in range(4)] for r in range(4)]
    pulled = mv(tr(trans), read)
    wy = weight * obs
    vec_part = [wy * pulled[r] for r in range(4)]
    mat_part = [[weight * pulled[r] * pulled[c] for c in range(4)] for r in range(4)]
    flat = join_flat([trans_part, offset, cov_part, vec_part, mat_part])
    flat = prefix_rows(flat)
    for index, value in enumerate(flat):
        out_ref[index] = value
        sum_ref[index:index + 1, :] = value[steps - 1:steps]


def fold_filter(place, recv_refs):
    count = len(recv_refs) + 1
    mean = None
    cov = None
    for shift in range(count - 1, 0, -1):
        ref = recv_refs[shift - 1]
        element = split_flat([ref[index:index + 1, :] for index in range(56)], FILTER_SIZES)
        if mean is None:
            zero = jnp.zeros_like(element[1][0])
            mean = [zero] * 4
            cov = [[zero] * 4 for _ in range(4)]
        new_mean, new_cov = apply_filter(mean, cov, element)
        take = place >= shift
        mean = [jnp.where(take, a, b) for a, b in zip(new_mean, mean)]
        cov = [[jnp.where(take, a, b) for a, b in zip(ra, rb)] for ra, rb in zip(new_cov, cov)]
    return mean, cov


def fold_smooth(place, recv_refs):
    count = len(recv_refs) + 1
    mean = None
    cov = None
    for shift in range(count - 1, 0, -1):
        ref = recv_refs[shift - 1]
        element = split_flat([ref[index:index + 1, :] for index in range(36)], SMOOTH_SIZES)
        if mean is None:
            zero = jnp.zeros_like(element[1][0])
            mean = [zero] * 4
            cov = [[zero] * 4 for _ in range(4)]
        new_mean, new_cov = apply_smooth(mean, cov, element)
        take = place + shift <= count - 1
        mean = [jnp.where(take, a, b) for a, b in zip(new_mean, mean)]
        cov = [[jnp.where(take, a, b) for a, b in zip(ra, rb)] for ra, rb in zip(new_cov, cov)]
    return mean, cov


def middle_kernel(place_ref, pre_ref, keep_ref, rot_ref, fcov_ref, *rest):
    recv_refs = rest[:-2]
    out_ref, head_ref = rest[-2:]
    place = place_ref[0]
    enter_mean, enter_cov = fold_filter(place, recv_refs)
    element = split_flat([pre_ref[index] for index in range(56)], FILTER_SIZES)
    mean_f, cov_f = apply_filter(enter_mean, enter_cov, element)
    keep = keep_ref[...]
    rot = row_mat(rot_ref)
    fcov = cube_mat(fcov_ref)
    trans = [[keep * rot[r][c] for c in range(4)] for r in range(4)]
    fade = 1.0 - keep * keep
    noise = [[fade * fcov[r][c] for c in range(4)] for r in range(4)]
    trans_t = tr(trans)
    predicted = madd(mm(mm(trans, cov_f), trans_t), noise)
    steps, modes = keep.shape
    row = lax.broadcasted_iota(jnp.int32, (steps, modes), 0)
    count = len(recv_refs) + 1
    live = jnp.where((row == steps - 1) & (place == count - 1), 0.0, 1.0)
    gain = mm(mm(cov_f, trans_t), inv4(predicted))
    gain = [[gain[r][c] * live for c in range(4)] for r in range(4)]
    pushed = mv(gain, mv(trans, mean_f))
    offset = [mean_f[r] - pushed[r] for r in range(4)]
    taken = mm(mm(gain, trans), cov_f)
    resid = [[cov_f[r][c] - taken[r][c] for c in range(4)] for r in range(4)]
    flat = suffix_rows(join_flat([gain, offset, resid]))
    for index, value in enumerate(flat):
        out_ref[index] = value
        head_ref[index:index + 1, :] = value[0:1]


def final_kernel(place_ref, suf_ref, read_ref, *rest):
    recv_refs = rest[:-2]
    mean_ref, spread_ref = rest[-2:]
    place = place_ref[0]
    leave_mean, leave_cov = fold_smooth(place, recv_refs)
    element = split_flat([suf_ref[index] for index in range(36)], SMOOTH_SIZES)
    mean_s, cov_s = apply_smooth(leave_mean, leave_cov, element)
    read = [read_ref[r:r + 1, :] for r in range(4)]
    for r in range(4):
        mean_ref[:, r, :] = mean_s[r]
    proj = mv(cov_s, read)
    total = read[0] * proj[0] + read[1] * proj[1] + read[2] * proj[2] + read[3] * proj[3]
    spread_ref[...] = jnp.log(total)


def run_kernel(kernel, out_shapes, smem_count, *args):
    specs = [pl.BlockSpec(memory_space=pltpu.SMEM)] * smem_count
    specs += [pl.BlockSpec(memory_space=pltpu.VMEM)] * (len(args) - smem_count)
    return pl.pallas_call(kernel, out_shape=out_shapes, in_specs=specs, interpret=INTERPRET)(*args)


def rotation_flat(angles):
    mode_count = angles.shape[-1]
    one = jnp.ones((mode_count,), angles.dtype)
    zero = jnp.zeros((mode_count,), angles.dtype)
    result = eye4(one, zero)
    planes = ((0, 1), (2, 3), (1, 2), (0, 3))
    for plane_index in range(4):
        first, second = planes[plane_index]
        cos_value = jnp.cos(angles[plane_index])
        sin_value = jnp.sin(angles[plane_index])
        rotate = eye4(one, zero)
        rotate[first][first] = cos_value
        rotate[second][second] = cos_value
        rotate[first][second] = -sin_value
        rotate[second][first] = sin_value
        result = mm(rotate, result)
    return jnp.stack(from_mat(result), axis=0)


def exchange(summary, forward):
    count = lax.axis_size("tm")
    received = []
    for shift in range(1, count):
        if forward:
            pairs = [(i, (i + shift) % count) for i in range(count)]
        else:
            pairs = [(i, (i - shift) % count) for i in range(count)]
        received.append(lax.ppermute(summary, "tm", pairs))
    return received


def local(
    readings, seen_mask, sensor, time_gaps, noise_var, readout, angles, decay_rates, field_cov
):
    real_type = readings.dtype
    steps_here = readings.shape[0]
    mode_count = readings.shape[1]
    place = jnp.reshape(lax.axis_index("tm"), (1,)).astype(jnp.int32)
    decay = decay_rates.reshape(1, mode_count)
    prefix, summary, rot, retain_next = run_kernel(
        filter_kernel,
        (
            jax.ShapeDtypeStruct((56, steps_here, mode_count), real_type),
            jax.ShapeDtypeStruct((56, mode_count), real_type),
            jax.ShapeDtypeStruct((16, mode_count), real_type),
            jax.ShapeDtypeStruct((steps_here, mode_count), real_type),
        ),
        3,
        place, time_gaps, sensor, readings, seen_mask, noise_var, readout, angles, decay, field_cov,
    )
    received = exchange(summary, True)
    suffix, head = run_kernel(
        middle_kernel,
        (
            jax.ShapeDtypeStruct((36, steps_here, mode_count), real_type),
            jax.ShapeDtypeStruct((36, mode_count), real_type),
        ),
        1,
        place, prefix, retain_next, rot, field_cov, *received,
    )
    received_back = exchange(head, False)
    mean_out, log_spread = run_kernel(
        final_kernel,
        (
            jax.ShapeDtypeStruct((steps_here, 4, mode_count), real_type),
            jax.ShapeDtypeStruct((steps_here, mode_count), real_type),
        ),
        1,
        place, suffix, readout, *received_back,
    )
    return (mean_out, log_spread)


def solution(mesh):
    return jax.shard_map(
        local,
        mesh=mesh,
        in_specs=(
            P("tm", "ens"),
            P("tm", None),
            P("tm"),
            P(),
            P(None, "ens"),
            P(None, "ens"),
            P(None, "ens"),
            P("ens"),
            P(None, None, "ens"),
        ),
        out_specs=(P("tm", None, "ens"), P("tm", "ens")),
        check_vma=False,
    )
```

```python
import jax
import jax.numpy as jnp
from jax import lax
from jax.experimental import pallas as pl
from jax.experimental.pallas import tpu as pltpu
from jax.sharding import PartitionSpec as P

INTERPRET = False
FILTER_SIZES = (16, 4, 16, 4, 16)
SMOOTH_SIZES = (16, 4, 16)


def eye4(one, zero):
    return [[one if row == col else zero for col in range(4)] for row in range(4)]


def mm(left, right):
    return [
        [
            left[row][0] * right[0][col]
            + left[row][1] * right[1][col]
            + left[row][2] * right[2][col]
            + left[row][3] * right[3][col]
            for col in range(4)
        ]
        for row in range(4)
    ]


def mv(matrix, vector):
    return [
        matrix[row][0] * vector[0]
        + matrix[row][1] * vector[1]
        + matrix[row][2] * vector[2]
        + matrix[row][3] * vector[3]
        for row in range(4)
    ]


def tr(matrix):
    return [[matrix[col][row] for col in range(4)] for row in range(4)]


def madd(left, right):
    return [[left[row][col] + right[row][col] for col in range(4)] for row in range(4)]


def vadd(left, right):
    return [left[row] + right[row] for row in range(4)]


def det3(rows):
    return (
        rows[0][0] * (rows[1][1] * rows[2][2] - rows[1][2] * rows[2][1])
        - rows[0][1] * (rows[1][0] * rows[2][2] - rows[1][2] * rows[2][0])
        + rows[0][2] * (rows[1][0] * rows[2][1] - rows[1][1] * rows[2][0])
    )


def inv4(matrix):
    cof = []
    for row_skip in range(4):
        line = []
        for col_skip in range(4):
            minor = [
                [matrix[r][c] for c in range(4) if c != col_skip] for r in range(4) if r != row_skip
            ]
            value = det3(minor)
            line.append(value if (row_skip + col_skip) % 2 == 0 else -value)
        cof.append(line)
    det = matrix[0][0] * cof[0][0]
    for col in range(1, 4):
        det = det + matrix[0][col] * cof[0][col]
    scale = 1.0 / det
    return [[cof[col][row] * scale for col in range(4)] for row in range(4)]


def to_mat(flat):
    return [[flat[4 * row + col] for col in range(4)] for row in range(4)]


def from_mat(matrix):
    return [matrix[row][col] for row in range(4) for col in range(4)]


def split_flat(flat, sizes):
    parts = []
    offset = 0
    for size in sizes:
        piece = flat[offset:offset + size]
        parts.append(to_mat(piece) if size == 16 else list(piece))
        offset += size
    return parts


def join_flat(parts):
    flat = []
    for part in parts:
        flat.extend(from_mat(part) if isinstance(part[0], list) else part)
    return flat


def filter_combine(first, second):
    trans_i, mean_i, cov_i, vec_i, mat_i = first
    trans_j, mean_j, cov_j, vec_j, mat_j = second
    one = jnp.ones_like(cov_i[0][0])
    zero = jnp.zeros_like(cov_i[0][0])
    mixing = inv4(madd(eye4(one, zero), mm(cov_i, mat_j)))
    carried = mm(trans_j, mixing)
    mean_part = vadd(mv(carried, vadd(mean_i, mv(cov_i, vec_j))), mean_j)
    cov_part = madd(mm(mm(carried, cov_i), tr(trans_j)), cov_j)
    trans_part = mm(carried, trans_i)
    pulled = tr(mm(mixing, trans_i))
    resid = [vec_j[row] - value for row, value in enumerate(mv(mat_j, mean_i))]
    vec_part = vadd(mv(pulled, resid), vec_i)
    mat_part = madd(mm(mm(pulled, mat_j), trans_i), mat_i)
    return [trans_part, mean_part, cov_part, vec_part, mat_part]


def apply_filter(mean_in, cov_in, element):
    trans_j, mean_j, cov_j, vec_j, mat_j = element
    one = jnp.ones_like(cov_j[0][0])
    zero = jnp.zeros_like(cov_j[0][0])
    mixing = inv4(madd(eye4(one, zero), mm(cov_in, mat_j)))
    carried = mm(trans_j, mixing)
    mean_part = vadd(mv(carried, vadd(mean_in, mv(cov_in, vec_j))), mean_j)
    cov_part = madd(mm(mm(carried, cov_in), tr(trans_j)), cov_j)
    return mean_part, cov_part


def smooth_compose(earlier, later):
    gain_e, mean_e, cov_e = earlier
    gain_l, mean_l, cov_l = later
    mean_part = vadd(mv(gain_e, mean_l), mean_e)
    cov_part = madd(mm(mm(gain_e, cov_l), tr(gain_e)), cov_e)
    return [mm(gain_e, gain_l), mean_part, cov_part]


def apply_smooth(mean_in, cov_in, element):
    gain, mean_e, cov_e = element
    mean_part = vadd(mv(gain, mean_in), mean_e)
    cov_part = madd(mm(mm(gain, cov_in), tr(gain)), cov_e)
    return mean_part, cov_part


def identity_flat(sizes, like):
    one = jnp.ones_like(like)
    zero = jnp.zeros_like(like)
    flat = []
    for slot, size in enumerate(sizes):
        if slot == 0:
            flat.extend(from_mat(eye4(one, zero)))
        else:
            flat.extend([zero] * size)
    return flat


def shift_rows(flat, ident, shift, forward):
    count = flat[0].shape[0]
    row = lax.broadcasted_iota(jnp.int32, flat[0].shape, 0)
    out = []
    for value, pad in zip(flat, ident):
        if forward:
            moved = pltpu.roll(value, shift, 0)
            out.append(jnp.where(row >= shift, moved, pad))
        else:
            moved = pltpu.roll(value, count - shift, 0)
            out.append(jnp.where(row < count - shift, moved, pad))
    return out


def prefix_rows(flat):
    count = flat[0].shape[0]
    ident = identity_flat(FILTER_SIZES, flat[0])
    shift = 1
    while shift < count:
        earlier = shift_rows(flat, ident, shift, True)
        flat = join_flat(
            filter_combine(split_flat(earlier, FILTER_SIZES), split_flat(flat, FILTER_SIZES))
        )
        shift *= 2
    return flat


def suffix_rows(flat):
    count = flat[0].shape[0]
    ident = identity_flat(SMOOTH_SIZES, flat[0])
    shift = 1
    while shift < count:
        later = shift_rows(flat, ident, shift, False)
        flat = join_flat(
            smooth_compose(split_flat(flat, SMOOTH_SIZES), split_flat(later, SMOOTH_SIZES))
        )
        shift *= 2
    return flat


def tree_rows(flat, scratch_ref, sizes, combine):
    rows, modes = flat[0].shape
    span = rows
    chunks = modes // 128
    block = len(flat) * span
    while rows > 1:
        half = rows // 2
        for index, value in enumerate(flat):
            for part in range(chunks):
                base = part * block + index * span
                scratch_ref[base:base + rows, :] = value[:, part * 128:(part + 1) * 128]
        even = []
        odd = []
        for index in range(len(flat)):
            pieces_even = []
            pieces_odd = []
            for part in range(chunks):
                base = part * block + index * span
                pieces_even.append(scratch_ref[pl.ds(base, half, stride=2), :])
                pieces_odd.append(scratch_ref[pl.ds(base + 1, half, stride=2), :])
            even.append(jnp.concatenate(pieces_even, axis=1) if chunks > 1 else pieces_even[0])
            odd.append(jnp.concatenate(pieces_odd, axis=1) if chunks > 1 else pieces_odd[0])
        flat = join_flat(combine(split_flat(even, sizes), split_flat(odd, sizes)))
        rows = half
    return flat


def prefix_kernel(elem_ref, out_ref):
    flat = prefix_rows([elem_ref[index] for index in range(56)])
    for index, value in enumerate(flat):
        out_ref[index] = value


def suffix_kernel(elem_ref, out_ref):
    flat = suffix_rows([elem_ref[index] for index in range(36)])
    for index, value in enumerate(flat):
        out_ref[index] = value


def row_mat(ref):
    return [[ref[4 * r + c:4 * r + c + 1, :] for c in range(4)] for r in range(4)]


def cube_mat(ref):
    return [[ref[r, c:c + 1, :] for c in range(4)] for r in range(4)]


def filter_kernel(
    place_ref, gaps_ref, sensor_ref, obs_ref, seen_ref, noise_ref, read_ref, angle_ref, decay_ref,
    fcov_ref, out_ref, sum_ref, rot_ref, next_ref, scratch_ref,
):
    steps, modes = obs_ref.shape
    total = gaps_ref.shape[0]
    start = place_ref[0] * steps
    row = lax.broadcasted_iota(jnp.int32, (steps, modes), 0)
    zero = jnp.zeros((steps, modes), jnp.float32)
    gap_here = zero
    gap_next = zero
    step_var = zero
    for k in range(steps):
        here = row == k
        gap_here = jnp.where(here, gaps_ref[start + k], gap_here)
        later = jnp.minimum(start + k + 1, total - 1)
        gap_next = jnp.where(here & (start + k + 1 < total), gaps_ref[later], gap_next)
        step_var = jnp.where(here, noise_ref[pl.ds(sensor_ref[k], 1), :], step_var)
    decay = decay_ref[...]
    keep = jnp.where(row + start > 0, jnp.exp(-decay * gap_here), 0.0)
    next_ref[...] = jnp.exp(-decay * gap_next)
    one = jnp.ones((1, modes), jnp.float32)
    flat_zero = jnp.zeros((1, modes), jnp.float32)
    rot = eye4(one, flat_zero)
    planes = ((0, 1), (2, 3), (1, 2), (0, 3))
    for plane_index in range(4):
        first, second = planes[plane_index]
        angle = angle_ref[plane_index:plane_index + 1, :]
        cos_value = jnp.cos(angle)
        sin_value = jnp.sin(angle)
        rotate = eye4(one, flat_zero)
        rotate[first][first] = cos_value
        rotate[second][second] = cos_value
        rotate[first][second] = -sin_value
        rotate[second][first] = sin_value
        rot = mm(rotate, rot)
    for index, value in enumerate(from_mat(rot)):
        rot_ref[index:index + 1, :] = value
    obs = obs_ref[...]
    seen = seen_ref[...].astype(obs.dtype)
    fcov = cube_mat(fcov_ref)
    read = [read_ref[r:r + 1, :] for r in range(4)]
    trans = [[keep * rot[r][c] for c in range(4)] for r in range(4)]
    fade = 1.0 - keep * keep
    noise = [[fade * fcov[r][c] for c in range(4)] for r in range(4)]
    spread = mv(noise, read)
    innov = (
        read[0] * spread[0] + read[1] * spread[1] + read[2] * spread[2] + read[3] * spread[3]
    ) + step_var
    weight = seen / innov
    gain = [weight * spread[r] for r in range(4)]
    shrink = [
        [(1.0 if r == c else 0.0) - gain[r] * read[c] for c in range(4)] for r in range(4)
    ]
    trans_part = mm(shrink, trans)
    offset = [gain[r] * obs for r in range(4)]
    cov_part = [[noise[r][c] - weight * spread[r] * spread[c] for c in range(4)] for r in range(4)]
    pulled = mv(tr(trans), read)
    wy = weight * obs
    vec_part = [wy * pulled[r] for r in range(4)]
    mat_part = [[weight * pulled[r] * pulled[c] for c in range(4)] for r in range(4)]
    flat = join_flat([trans_part, offset, cov_part, vec_part, mat_part])
    for index, value in enumerate(flat):
        out_ref[index] = value
    total_flat = tree_rows(flat, scratch_ref, FILTER_SIZES, filter_combine)
    for index, value in enumerate(total_flat):
        sum_ref[index:index + 1, :] = value


def fold_filter(place, recv_refs):
    count = len(recv_refs) + 1
    mean = None
    cov = None
    for shift in range(count - 1, 0, -1):
        ref = recv_refs[shift - 1]
        element = split_flat([ref[index:index + 1, :] for index in range(56)], FILTER_SIZES)
        if mean is None:
            zero = jnp.zeros_like(element[1][0])
            mean = [zero] * 4
            cov = [[zero] * 4 for _ in range(4)]
        new_mean, new_cov = apply_filter(mean, cov, element)
        take = place >= shift
        mean = [jnp.where(take, a, b) for a, b in zip(new_mean, mean)]
        cov = [[jnp.where(take, a, b) for a, b in zip(ra, rb)] for ra, rb in zip(new_cov, cov)]
    return mean, cov


def fold_smooth(place, recv_refs):
    count = len(recv_refs) + 1
    mean = None
    cov = None
    for shift in range(count - 1, 0, -1):
        ref = recv_refs[shift - 1]
        element = split_flat([ref[index:index + 1, :] for index in range(36)], SMOOTH_SIZES)
        if mean is None:
            zero = jnp.zeros_like(element[1][0])
            mean = [zero] * 4
            cov = [[zero] * 4 for _ in range(4)]
        new_mean, new_cov = apply_smooth(mean, cov, element)
        take = place + shift <= count - 1
        mean = [jnp.where(take, a, b) for a, b in zip(new_mean, mean)]
        cov = [[jnp.where(take, a, b) for a, b in zip(ra, rb)] for ra, rb in zip(new_cov, cov)]
    return mean, cov

def middle_kernel(place_ref, pre_ref, keep_ref, rot_ref, fcov_ref, *rest):
    out_ref, head_ref, scratch_ref = rest[-3:]
    recv_refs = rest[:-3]
    place = place_ref[0]
    enter_mean, enter_cov = fold_filter(place, recv_refs)
    element = split_flat([pre_ref[index] for index in range(56)], FILTER_SIZES)
    mean_f, cov_f = apply_filter(enter_mean, enter_cov, element)
    keep = keep_ref[...]
    rot = row_mat(rot_ref)
    fcov = cube_mat(fcov_ref)
    trans = [[keep * rot[r][c] for c in range(4)] for r in range(4)]
    fade = 1.0 - keep * keep
    noise = [[fade * fcov[r][c] for c in range(4)] for r in range(4)]
    trans_t = tr(trans)
    predicted = madd(mm(mm(trans, cov_f), trans_t), noise)
    steps, modes = keep.shape
    row = lax.broadcasted_iota(jnp.int32, (steps, modes), 0)
    count = len(recv_refs) + 1
    live = jnp.where((row == steps - 1) & (place == count - 1), 0.0, 1.0)
    gain = mm(mm(cov_f, trans_t), inv4(predicted))
    gain = [[gain[r][c] * live for c in range(4)] for r in range(4)]
    pushed = mv(gain, mv(trans, mean_f))
    offset = [mean_f[r] - pushed[r] for r in range(4)]
    taken = mm(mm(gain, trans), cov_f)
    resid = [[cov_f[r][c] - taken[r][c] for c in range(4)] for r in range(4)]
    flat = join_flat([gain, offset, resid])
    for index, value in enumerate(flat):
        out_ref[index] = value
    total_flat = tree_rows(flat, scratch_ref, SMOOTH_SIZES, smooth_compose)
    for index, value in enumerate(total_flat):
        head_ref[index:index + 1, :] = value


def final_kernel(place_ref, suf_ref, read_ref, *rest):
    recv_refs = rest[:-2]
    mean_ref, spread_ref = rest[-2:]
    place = place_ref[0]
    leave_mean, leave_cov = fold_smooth(place, recv_refs)
    element = split_flat([suf_ref[index] for index in range(36)], SMOOTH_SIZES)
    mean_s, cov_s = apply_smooth(leave_mean, leave_cov, element)
    read = [read_ref[r:r + 1, :] for r in range(4)]
    for r in range(4):
        mean_ref[:, r, :] = mean_s[r]
    proj = mv(cov_s, read)
    total = read[0] * proj[0] + read[1] * proj[1] + read[2] * proj[2] + read[3] * proj[3]
    spread_ref[...] = jnp.log(total)


def run_kernel(kernel, out_shapes, smem_count, *args, scratch=()):
    specs = [pl.BlockSpec(memory_space=pltpu.SMEM)] * smem_count
    specs += [pl.BlockSpec(memory_space=pltpu.VMEM)] * (len(args) - smem_count)
    return pl.pallas_call(
        kernel, out_shape=out_shapes, in_specs=specs, scratch_shapes=scratch, interpret=INTERPRET
    )(*args)


def rotation_flat(angles):
    mode_count = angles.shape[-1]
    one = jnp.ones((mode_count,), angles.dtype)
    zero = jnp.zeros((mode_count,), angles.dtype)
    result = eye4(one, zero)
    planes = ((0, 1), (2, 3), (1, 2), (0, 3))
    for plane_index in range(4):
        first, second = planes[plane_index]
        cos_value = jnp.cos(angles[plane_index])
        sin_value = jnp.sin(angles[plane_index])
        rotate = eye4(one, zero)
        rotate[first][first] = cos_value
        rotate[second][second] = cos_value
        rotate[first][second] = -sin_value
        rotate[second][first] = sin_value
        result = mm(rotate, result)
    return jnp.stack(from_mat(result), axis=0)


def exchange(summary, forward):
    count = lax.axis_size("tm")
    received = []
    for shift in range(1, count):
        if forward:
            pairs = [(i, (i + shift) % count) for i in range(count)]
        else:
            pairs = [(i, (i - shift) % count) for i in range(count)]
        received.append(lax.ppermute(summary, "tm", pairs))
    return received


def local(
    readings, seen_mask, sensor, time_gaps, noise_var, readout, angles, decay_rates, field_cov
):
    real_type = readings.dtype
    steps_here = readings.shape[0]
    mode_count = readings.shape[1]
    place = jnp.reshape(lax.axis_index("tm"), (1,)).astype(jnp.int32)
    decay = decay_rates.reshape(1, mode_count)
    elements, summary, rot, retain_next = run_kernel(
        filter_kernel,
        (
            jax.ShapeDtypeStruct((56, steps_here, mode_count), real_type),
            jax.ShapeDtypeStruct((56, mode_count), real_type),
            jax.ShapeDtypeStruct((16, mode_count), real_type),
            jax.ShapeDtypeStruct((steps_here, mode_count), real_type),
        ),
        3,
        place, time_gaps, sensor, readings, seen_mask, noise_var, readout, angles, decay, field_cov,
        scratch=[pltpu.VMEM((56 * steps_here * (mode_count // 128), 128), real_type)],
    )
    received = exchange(summary, True)
    prefix = run_kernel(
        prefix_kernel, jax.ShapeDtypeStruct((56, steps_here, mode_count), real_type), 0, elements
    )
    smooth_elems, head = run_kernel(
        middle_kernel,
        (
            jax.ShapeDtypeStruct((36, steps_here, mode_count), real_type),
            jax.ShapeDtypeStruct((36, mode_count), real_type),
        ),
        1,
        place, prefix, retain_next, rot, field_cov, *received,
        scratch=[pltpu.VMEM((36 * steps_here * (mode_count // 128), 128), real_type)],
    )
    received_back = exchange(head, False)
    suffix = run_kernel(
        suffix_kernel, jax.ShapeDtypeStruct((36, steps_here, mode_count), real_type), 0, smooth_elems
    )
    mean_out, log_spread = run_kernel(
        final_kernel,
        (
            jax.ShapeDtypeStruct((steps_here, 4, mode_count), real_type),
            jax.ShapeDtypeStruct((steps_here, mode_count), real_type),
        ),
        1,
        place, suffix, readout, *received_back,
    )
    return (mean_out, log_spread)


def solution(mesh):
    return jax.shard_map(
        local,
        mesh=mesh,
        in_specs=(
            P("tm", "ens"),
            P("tm", None),
            P("tm"),
            P(),
            P(None, "ens"),
            P(None, "ens"),
            P(None, "ens"),
            P("ens"),
            P(None, None, "ens"),
        ),
        out_specs=(P("tm", None, "ens"), P("tm", "ens")),
        check_vma=False,
    )
```

```python
import jax
import jax.numpy as jnp
from jax import lax
from jax.experimental import pallas as pl
from jax.experimental.pallas import tpu as pltpu
from jax.sharding import PartitionSpec as P

INTERPRET = False
FILTER_SIZES = (16, 4, 16, 4, 16)
SMOOTH_SIZES = (16, 4, 16)


def eye4(one, zero):
    return [[one if row == col else zero for col in range(4)] for row in range(4)]


def mm(left, right):
    return [
        [
            left[row][0] * right[0][col]
            + left[row][1] * right[1][col]
            + left[row][2] * right[2][col]
            + left[row][3] * right[3][col]
            for col in range(4)
        ]
        for row in range(4)
    ]


def mv(matrix, vector):
    return [
        matrix[row][0] * vector[0]
        + matrix[row][1] * vector[1]
        + matrix[row][2] * vector[2]
        + matrix[row][3] * vector[3]
        for row in range(4)
    ]


def tr(matrix):
    return [[matrix[col][row] for col in range(4)] for row in range(4)]


def madd(left, right):
    return [[left[row][col] + right[row][col] for col in range(4)] for row in range(4)]


def vadd(left, right):
    return [left[row] + right[row] for row in range(4)]


def det3(rows):
    return (
        rows[0][0] * (rows[1][1] * rows[2][2] - rows[1][2] * rows[2][1])
        - rows[0][1] * (rows[1][0] * rows[2][2] - rows[1][2] * rows[2][0])
        + rows[0][2] * (rows[1][0] * rows[2][1] - rows[1][1] * rows[2][0])
    )


def inv4(matrix):
    cof = []
    for row_skip in range(4):
        line = []
        for col_skip in range(4):
            minor = [
                [matrix[r][c] for c in range(4) if c != col_skip] for r in range(4) if r != row_skip
            ]
            value = det3(minor)
            line.append(value if (row_skip + col_skip) % 2 == 0 else -value)
        cof.append(line)
    det = matrix[0][0] * cof[0][0]
    for col in range(1, 4):
        det = det + matrix[0][col] * cof[0][col]
    scale = 1.0 / det
    return [[cof[col][row] * scale for col in range(4)] for row in range(4)]


def to_mat(flat):
    return [[flat[4 * row + col] for col in range(4)] for row in range(4)]


def from_mat(matrix):
    return [matrix[row][col] for row in range(4) for col in range(4)]


def split_flat(flat, sizes):
    parts = []
    offset = 0
    for size in sizes:
        piece = flat[offset:offset + size]
        parts.append(to_mat(piece) if size == 16 else list(piece))
        offset += size
    return parts


def join_flat(parts):
    flat = []
    for part in parts:
        flat.extend(from_mat(part) if isinstance(part[0], list) else part)
    return flat


def filter_combine(first, second):
    trans_i, mean_i, cov_i, vec_i, mat_i = first
    trans_j, mean_j, cov_j, vec_j, mat_j = second
    one = jnp.ones_like(cov_i[0][0])
    zero = jnp.zeros_like(cov_i[0][0])
    mixing = inv4(madd(eye4(one, zero), mm(cov_i, mat_j)))
    carried = mm(trans_j, mixing)
    mean_part = vadd(mv(carried, vadd(mean_i, mv(cov_i, vec_j))), mean_j)
    cov_part = madd(mm(mm(carried, cov_i), tr(trans_j)), cov_j)
    trans_part = mm(carried, trans_i)
    pulled = tr(mm(mixing, trans_i))
    resid = [vec_j[row] - value for row, value in enumerate(mv(mat_j, mean_i))]
    vec_part = vadd(mv(pulled, resid), vec_i)
    mat_part = madd(mm(mm(pulled, mat_j), trans_i), mat_i)
    return [trans_part, mean_part, cov_part, vec_part, mat_part]


def apply_filter(mean_in, cov_in, element):
    trans_j, mean_j, cov_j, vec_j, mat_j = element
    one = jnp.ones_like(cov_j[0][0])
    zero = jnp.zeros_like(cov_j[0][0])
    mixing = inv4(madd(eye4(one, zero), mm(cov_in, mat_j)))
    carried = mm(trans_j, mixing)
    mean_part = vadd(mv(carried, vadd(mean_in, mv(cov_in, vec_j))), mean_j)
    cov_part = madd(mm(mm(carried, cov_in), tr(trans_j)), cov_j)
    return mean_part, cov_part


def smooth_compose(earlier, later):
    gain_e, mean_e, cov_e = earlier
    gain_l, mean_l, cov_l = later
    mean_part = vadd(mv(gain_e, mean_l), mean_e)
    cov_part = madd(mm(mm(gain_e, cov_l), tr(gain_e)), cov_e)
    return [mm(gain_e, gain_l), mean_part, cov_part]


def apply_smooth(mean_in, cov_in, element):
    gain, mean_e, cov_e = element
    mean_part = vadd(mv(gain, mean_in), mean_e)
    cov_part = madd(mm(mm(gain, cov_in), tr(gain)), cov_e)
    return mean_part, cov_part


def identity_flat(sizes, like):
    one = jnp.ones_like(like)
    zero = jnp.zeros_like(like)
    flat = []
    for slot, size in enumerate(sizes):
        if slot == 0:
            flat.extend(from_mat(eye4(one, zero)))
        else:
            flat.extend([zero] * size)
    return flat


def shift_rows(flat, ident, shift, forward):
    count = flat[0].shape[0]
    row = lax.broadcasted_iota(jnp.int32, flat[0].shape, 0)
    out = []
    for value, pad in zip(flat, ident):
        if forward:
            moved = pltpu.roll(value, shift, 0)
            out.append(jnp.where(row >= shift, moved, pad))
        else:
            moved = pltpu.roll(value, count - shift, 0)
            out.append(jnp.where(row < count - shift, moved, pad))
    return out


def prefix_rows(flat):
    count = flat[0].shape[0]
    ident = identity_flat(FILTER_SIZES, flat[0])
    shift = 1
    while shift < count:
        earlier = shift_rows(flat, ident, shift, True)
        flat = join_flat(
            filter_combine(split_flat(earlier, FILTER_SIZES), split_flat(flat, FILTER_SIZES))
        )
        shift *= 2
    return flat


def suffix_rows(flat):
    count = flat[0].shape[0]
    ident = identity_flat(SMOOTH_SIZES, flat[0])
    shift = 1
    while shift < count:
        later = shift_rows(flat, ident, shift, False)
        flat = join_flat(
            smooth_compose(split_flat(flat, SMOOTH_SIZES), split_flat(later, SMOOTH_SIZES))
        )
        shift *= 2
    return flat


def tree_rows(flat, scratch_ref, sizes, combine):
    rows, modes = flat[0].shape
    span = rows
    chunks = modes // 128
    block = len(flat) * span
    while rows > 1:
        half = rows // 2
        for index, value in enumerate(flat):
            for part in range(chunks):
                base = part * block + index * span
                scratch_ref[base:base + rows, :] = value[:, part * 128:(part + 1) * 128]
        even = []
        odd = []
        for index in range(len(flat)):
            pieces_even = []
            pieces_odd = []
            for part in range(chunks):
                base = part * block + index * span
                pieces_even.append(scratch_ref[pl.ds(base, half, stride=2), :])
                pieces_odd.append(scratch_ref[pl.ds(base + 1, half, stride=2), :])
            even.append(jnp.concatenate(pieces_even, axis=1) if chunks > 1 else pieces_even[0])
            odd.append(jnp.concatenate(pieces_odd, axis=1) if chunks > 1 else pieces_odd[0])
        flat = join_flat(combine(split_flat(even, sizes), split_flat(odd, sizes)))
        rows = half
    return flat


def prefix_kernel(elem_ref, out_ref):
    flat = prefix_rows([elem_ref[index] for index in range(56)])
    for index, value in enumerate(flat):
        out_ref[index] = value


def suffix_kernel(elem_ref, out_ref):
    flat = suffix_rows([elem_ref[index] for index in range(36)])
    for index, value in enumerate(flat):
        out_ref[index] = value


def row_mat(ref):
    return [[ref[4 * r + c:4 * r + c + 1, :] for c in range(4)] for r in range(4)]


def cube_mat(ref):
    return [[ref[r, c:c + 1, :] for c in range(4)] for r in range(4)]


def filter_kernel(
    place_ref, gaps_ref, sensor_ref, obs_ref, seen_ref, noise_ref, read_ref, angle_ref, decay_ref,
    fcov_ref, out_ref, sum_ref, rot_ref, next_ref, scratch_ref,
):
    steps, modes = obs_ref.shape
    total = gaps_ref.shape[0]
    start = place_ref[0] * steps
    row = lax.broadcasted_iota(jnp.int32, (steps, modes), 0)
    zero = jnp.zeros((steps, modes), jnp.float32)
    gap_here = zero
    gap_next = zero
    step_var = zero
    for k in range(steps):
        here = row == k
        gap_here = jnp.where(here, gaps_ref[start + k], gap_here)
        later = jnp.minimum(start + k + 1, total - 1)
        gap_next = jnp.where(here & (start + k + 1 < total), gaps_ref[later], gap_next)
        step_var = jnp.where(here, noise_ref[pl.ds(sensor_ref[k], 1), :], step_var)
    decay = decay_ref[...]
    keep = jnp.where(row + start > 0, jnp.exp(-decay * gap_here), 0.0)
    next_ref[...] = jnp.exp(-decay * gap_next)
    one = jnp.ones((1, modes), jnp.float32)
    flat_zero = jnp.zeros((1, modes), jnp.float32)
    rot = eye4(one, flat_zero)
    planes = ((0, 1), (2, 3), (1, 2), (0, 3))
    for plane_index in range(4):
        first, second = planes[plane_index]
        angle = angle_ref[plane_index:plane_index + 1, :]
        cos_value = jnp.cos(angle)
        sin_value = jnp.sin(angle)
        rotate = eye4(one, flat_zero)
        rotate[first][first] = cos_value
        rotate[second][second] = cos_value
        rotate[first][second] = -sin_value
        rotate[second][first] = sin_value
        rot = mm(rotate, rot)
    for index, value in enumerate(from_mat(rot)):
        rot_ref[index:index + 1, :] = value
    obs = obs_ref[...]
    seen = seen_ref[...].astype(obs.dtype)
    fcov = cube_mat(fcov_ref)
    read = [read_ref[r:r + 1, :] for r in range(4)]
    trans = [[keep * rot[r][c] for c in range(4)] for r in range(4)]
    fade = 1.0 - keep * keep
    noise = [[fade * fcov[r][c] for c in range(4)] for r in range(4)]
    spread = mv(noise, read)
    innov = (
        read[0] * spread[0] + read[1] * spread[1] + read[2] * spread[2] + read[3] * spread[3]
    ) + step_var
    weight = seen / innov
    gain = [weight * spread[r] for r in range(4)]
    shrink = [
        [(1.0 if r == c else 0.0) - gain[r] * read[c] for c in range(4)] for r in range(4)
    ]
    trans_part = mm(shrink, trans)
    offset = [gain[r] * obs for r in range(4)]
    cov_part = [[noise[r][c] - weight * spread[r] * spread[c] for c in range(4)] for r in range(4)]
    pulled = mv(tr(trans), read)
    wy = weight * obs
    vec_part = [wy * pulled[r] for r in range(4)]
    mat_part = [[weight * pulled[r] * pulled[c] for c in range(4)] for r in range(4)]
    flat = join_flat([trans_part, offset, cov_part, vec_part, mat_part])
    for index, value in enumerate(flat):
        out_ref[index] = value
    total_flat = tree_rows(flat, scratch_ref, FILTER_SIZES, filter_combine)
    for index, value in enumerate(total_flat):
        sum_ref[index:index + 1, :] = value


def fold_filter(place, recv_refs):
    count = len(recv_refs) + 1
    mean = None
    cov = None
    for shift in range(count - 1, 0, -1):
        ref = recv_refs[shift - 1]
        element = split_flat([ref[index:index + 1, :] for index in range(56)], FILTER_SIZES)
        if mean is None:
            zero = jnp.zeros_like(element[1][0])
            mean = [zero] * 4
            cov = [[zero] * 4 for _ in range(4)]
        new_mean, new_cov = apply_filter(mean, cov, element)
        take = place >= shift
        mean = [jnp.where(take, a, b) for a, b in zip(new_mean, mean)]
        cov = [[jnp.where(take, a, b) for a, b in zip(ra, rb)] for ra, rb in zip(new_cov, cov)]
    return mean, cov


def fold_smooth(place, recv_refs):
    count = len(recv_refs) + 1
    mean = None
    cov = None
    for shift in range(count - 1, 0, -1):
        ref = recv_refs[shift - 1]
        element = split_flat([ref[index:index + 1, :] for index in range(36)], SMOOTH_SIZES)
        if mean is None:
            zero = jnp.zeros_like(element[1][0])
            mean = [zero] * 4
            cov = [[zero] * 4 for _ in range(4)]
        new_mean, new_cov = apply_smooth(mean, cov, element)
        take = place + shift <= count - 1
        mean = [jnp.where(take, a, b) for a, b in zip(new_mean, mean)]
        cov = [[jnp.where(take, a, b) for a, b in zip(ra, rb)] for ra, rb in zip(new_cov, cov)]
    return mean, cov

def middle_kernel(place_ref, pre_ref, keep_ref, rot_ref, fcov_ref, *rest):
    out_ref, head_ref, scratch_ref, filt_ref = rest[-4:]
    recv_refs = rest[:-4]
    place = place_ref[0]
    mean_f, cov_f = fold_filter(place, recv_refs)
    steps = pre_ref.shape[1]
    for k in range(steps):
        element = split_flat([pre_ref[index, k:k + 1, :] for index in range(56)], FILTER_SIZES)
        mean_f, cov_f = apply_filter(mean_f, cov_f, element)
        for index, value in enumerate(join_flat([mean_f, cov_f])):
            filt_ref[index * steps + k:index * steps + k + 1, :] = value
    filt = [filt_ref[index * steps:(index + 1) * steps, :] for index in range(20)]
    mean_f = filt[:4]
    cov_f = to_mat(filt[4:])
    keep = keep_ref[...]
    rot = row_mat(rot_ref)
    fcov = cube_mat(fcov_ref)
    trans = [[keep * rot[r][c] for c in range(4)] for r in range(4)]
    fade = 1.0 - keep * keep
    noise = [[fade * fcov[r][c] for c in range(4)] for r in range(4)]
    trans_t = tr(trans)
    predicted = madd(mm(mm(trans, cov_f), trans_t), noise)
    steps, modes = keep.shape
    row = lax.broadcasted_iota(jnp.int32, (steps, modes), 0)
    count = len(recv_refs) + 1
    live = jnp.where((row == steps - 1) & (place == count - 1), 0.0, 1.0)
    gain = mm(mm(cov_f, trans_t), inv4(predicted))
    gain = [[gain[r][c] * live for c in range(4)] for r in range(4)]
    pushed = mv(gain, mv(trans, mean_f))
    offset = [mean_f[r] - pushed[r] for r in range(4)]
    taken = mm(mm(gain, trans), cov_f)
    resid = [[cov_f[r][c] - taken[r][c] for c in range(4)] for r in range(4)]
    flat = join_flat([gain, offset, resid])
    for index, value in enumerate(flat):
        out_ref[index] = value
    total_flat = tree_rows(flat, scratch_ref, SMOOTH_SIZES, smooth_compose)
    for index, value in enumerate(total_flat):
        head_ref[index:index + 1, :] = value


def final_kernel(place_ref, suf_ref, read_ref, *rest):
    recv_refs = rest[:-2]
    mean_ref, spread_ref = rest[-2:]
    place = place_ref[0]
    leave_mean, leave_cov = fold_smooth(place, recv_refs)
    element = split_flat([suf_ref[index] for index in range(36)], SMOOTH_SIZES)
    mean_s, cov_s = apply_smooth(leave_mean, leave_cov, element)
    read = [read_ref[r:r + 1, :] for r in range(4)]
    for r in range(4):
        mean_ref[:, r, :] = mean_s[r]
    proj = mv(cov_s, read)
    total = read[0] * proj[0] + read[1] * proj[1] + read[2] * proj[2] + read[3] * proj[3]
    spread_ref[...] = jnp.log(total)


def run_kernel(kernel, out_shapes, smem_count, *args, scratch=()):
    specs = [pl.BlockSpec(memory_space=pltpu.SMEM)] * smem_count
    specs += [pl.BlockSpec(memory_space=pltpu.VMEM)] * (len(args) - smem_count)
    return pl.pallas_call(
        kernel, out_shape=out_shapes, in_specs=specs, scratch_shapes=scratch, interpret=INTERPRET
    )(*args)


def rotation_flat(angles):
    mode_count = angles.shape[-1]
    one = jnp.ones((mode_count,), angles.dtype)
    zero = jnp.zeros((mode_count,), angles.dtype)
    result = eye4(one, zero)
    planes = ((0, 1), (2, 3), (1, 2), (0, 3))
    for plane_index in range(4):
        first, second = planes[plane_index]
        cos_value = jnp.cos(angles[plane_index])
        sin_value = jnp.sin(angles[plane_index])
        rotate = eye4(one, zero)
        rotate[first][first] = cos_value
        rotate[second][second] = cos_value
        rotate[first][second] = -sin_value
        rotate[second][first] = sin_value
        result = mm(rotate, result)
    return jnp.stack(from_mat(result), axis=0)


def exchange(summary, forward):
    count = lax.axis_size("tm")
    received = []
    for shift in range(1, count):
        if forward:
            pairs = [(i, (i + shift) % count) for i in range(count)]
        else:
            pairs = [(i, (i - shift) % count) for i in range(count)]
        received.append(lax.ppermute(summary, "tm", pairs))
    return received


def local(
    readings, seen_mask, sensor, time_gaps, noise_var, readout, angles, decay_rates, field_cov
):
    real_type = readings.dtype
    steps_here = readings.shape[0]
    mode_count = readings.shape[1]
    place = jnp.reshape(lax.axis_index("tm"), (1,)).astype(jnp.int32)
    decay = decay_rates.reshape(1, mode_count)
    elements, summary, rot, retain_next = run_kernel(
        filter_kernel,
        (
            jax.ShapeDtypeStruct((56, steps_here, mode_count), real_type),
            jax.ShapeDtypeStruct((56, mode_count), real_type),
            jax.ShapeDtypeStruct((16, mode_count), real_type),
            jax.ShapeDtypeStruct((steps_here, mode_count), real_type),
        ),
        3,
        place, time_gaps, sensor, readings, seen_mask, noise_var, readout, angles, decay, field_cov,
        scratch=[pltpu.VMEM((56 * steps_here * (mode_count // 128), 128), real_type)],
    )
    received = exchange(summary, True)
    smooth_elems, head = run_kernel(
        middle_kernel,
        (
            jax.ShapeDtypeStruct((36, steps_here, mode_count), real_type),
            jax.ShapeDtypeStruct((36, mode_count), real_type),
        ),
        1,
        place, elements, retain_next, rot, field_cov, *received,
        scratch=[
            pltpu.VMEM((36 * steps_here * (mode_count // 128), 128), real_type),
            pltpu.VMEM((20 * steps_here, mode_count), real_type),
        ],
    )
    received_back = exchange(head, False)
    suffix = run_kernel(
        suffix_kernel, jax.ShapeDtypeStruct((36, steps_here, mode_count), real_type), 0, smooth_elems
    )
    mean_out, log_spread = run_kernel(
        final_kernel,
        (
            jax.ShapeDtypeStruct((steps_here, 4, mode_count), real_type),
            jax.ShapeDtypeStruct((steps_here, mode_count), real_type),
        ),
        1,
        place, suffix, readout, *received_back,
    )
    return (mean_out, log_spread)


def solution(mesh):
    return jax.shard_map(
        local,
        mesh=mesh,
        in_specs=(
            P("tm", "ens"),
            P("tm", None),
            P("tm"),
            P(),
            P(None, "ens"),
            P(None, "ens"),
            P(None, "ens"),
            P("ens"),
            P(None, None, "ens"),
        ),
        out_specs=(P("tm", None, "ens"), P("tm", "ens")),
        check_vma=False,
    )
```

```python
import jax
import jax.numpy as jnp
from jax import lax
from jax.experimental import pallas as pl
from jax.experimental.pallas import tpu as pltpu
from jax.sharding import PartitionSpec as P

INTERPRET = False
FILTER_SIZES = (16, 4, 16, 4, 16)
SMOOTH_SIZES = (16, 4, 16)


def eye4(one, zero):
    return [[one if row == col else zero for col in range(4)] for row in range(4)]


def mm(left, right):
    return [
        [
            left[row][0] * right[0][col]
            + left[row][1] * right[1][col]
            + left[row][2] * right[2][col]
            + left[row][3] * right[3][col]
            for col in range(4)
        ]
        for row in range(4)
    ]


def mv(matrix, vector):
    return [
        matrix[row][0] * vector[0]
        + matrix[row][1] * vector[1]
        + matrix[row][2] * vector[2]
        + matrix[row][3] * vector[3]
        for row in range(4)
    ]


def tr(matrix):
    return [[matrix[col][row] for col in range(4)] for row in range(4)]


def madd(left, right):
    return [[left[row][col] + right[row][col] for col in range(4)] for row in range(4)]


def vadd(left, right):
    return [left[row] + right[row] for row in range(4)]


def det3(rows):
    return (
        rows[0][0] * (rows[1][1] * rows[2][2] - rows[1][2] * rows[2][1])
        - rows[0][1] * (rows[1][0] * rows[2][2] - rows[1][2] * rows[2][0])
        + rows[0][2] * (rows[1][0] * rows[2][1] - rows[1][1] * rows[2][0])
    )


def inv4(matrix):
    cof = []
    for row_skip in range(4):
        line = []
        for col_skip in range(4):
            minor = [
                [matrix[r][c] for c in range(4) if c != col_skip] for r in range(4) if r != row_skip
            ]
            value = det3(minor)
            line.append(value if (row_skip + col_skip) % 2 == 0 else -value)
        cof.append(line)
    det = matrix[0][0] * cof[0][0]
    for col in range(1, 4):
        det = det + matrix[0][col] * cof[0][col]
    scale = 1.0 / det
    return [[cof[col][row] * scale for col in range(4)] for row in range(4)]


def to_mat(flat):
    return [[flat[4 * row + col] for col in range(4)] for row in range(4)]


def from_mat(matrix):
    return [matrix[row][col] for row in range(4) for col in range(4)]


def split_flat(flat, sizes):
    parts = []
    offset = 0
    for size in sizes:
        piece = flat[offset:offset + size]
        parts.append(to_mat(piece) if size == 16 else list(piece))
        offset += size
    return parts


def join_flat(parts):
    flat = []
    for part in parts:
        flat.extend(from_mat(part) if isinstance(part[0], list) else part)
    return flat


def filter_combine(first, second):
    trans_i, mean_i, cov_i, vec_i, mat_i = first
    trans_j, mean_j, cov_j, vec_j, mat_j = second
    one = jnp.ones_like(cov_i[0][0])
    zero = jnp.zeros_like(cov_i[0][0])
    mixing = inv4(madd(eye4(one, zero), mm(cov_i, mat_j)))
    carried = mm(trans_j, mixing)
    mean_part = vadd(mv(carried, vadd(mean_i, mv(cov_i, vec_j))), mean_j)
    cov_part = madd(mm(mm(carried, cov_i), tr(trans_j)), cov_j)
    trans_part = mm(carried, trans_i)
    pulled = tr(mm(mixing, trans_i))
    resid = [vec_j[row] - value for row, value in enumerate(mv(mat_j, mean_i))]
    vec_part = vadd(mv(pulled, resid), vec_i)
    mat_part = madd(mm(mm(pulled, mat_j), trans_i), mat_i)
    return [trans_part, mean_part, cov_part, vec_part, mat_part]


def apply_filter(mean_in, cov_in, element):
    trans_j, mean_j, cov_j, vec_j, mat_j = element
    one = jnp.ones_like(cov_j[0][0])
    zero = jnp.zeros_like(cov_j[0][0])
    mixing = inv4(madd(eye4(one, zero), mm(cov_in, mat_j)))
    carried = mm(trans_j, mixing)
    mean_part = vadd(mv(carried, vadd(mean_in, mv(cov_in, vec_j))), mean_j)
    cov_part = madd(mm(mm(carried, cov_in), tr(trans_j)), cov_j)
    return mean_part, cov_part


def smooth_compose(earlier, later):
    gain_e, mean_e, cov_e = earlier
    gain_l, mean_l, cov_l = later
    mean_part = vadd(mv(gain_e, mean_l), mean_e)
    cov_part = madd(mm(mm(gain_e, cov_l), tr(gain_e)), cov_e)
    return [mm(gain_e, gain_l), mean_part, cov_part]


def apply_smooth(mean_in, cov_in, element):
    gain, mean_e, cov_e = element
    mean_part = vadd(mv(gain, mean_in), mean_e)
    cov_part = madd(mm(mm(gain, cov_in), tr(gain)), cov_e)
    return mean_part, cov_part


def identity_flat(sizes, like):
    one = jnp.ones_like(like)
    zero = jnp.zeros_like(like)
    flat = []
    for slot, size in enumerate(sizes):
        if slot == 0:
            flat.extend(from_mat(eye4(one, zero)))
        else:
            flat.extend([zero] * size)
    return flat


def shift_rows(flat, ident, shift, forward, block=None):
    count = flat[0].shape[0]
    row = lax.broadcasted_iota(jnp.int32, flat[0].shape, 0)
    if block is not None:
        row = row % block
    out = []
    for value, pad in zip(flat, ident):
        if forward:
            moved = pltpu.roll(value, shift, 0)
            out.append(jnp.where(row >= shift, moved, pad))
        else:
            moved = pltpu.roll(value, count - shift, 0)
            out.append(jnp.where(row < count - shift, moved, pad))
    return out


def prefix_rows(flat, block=None):
    count = flat[0].shape[0] if block is None else block
    ident = identity_flat(FILTER_SIZES, flat[0])
    shift = 1
    while shift < count:
        earlier = shift_rows(flat, ident, shift, True, block)
        flat = join_flat(
            filter_combine(split_flat(earlier, FILTER_SIZES), split_flat(flat, FILTER_SIZES))
        )
        shift *= 2
    return flat


def suffix_rows(flat):
    count = flat[0].shape[0]
    ident = identity_flat(SMOOTH_SIZES, flat[0])
    shift = 1
    while shift < count:
        later = shift_rows(flat, ident, shift, False)
        flat = join_flat(
            smooth_compose(split_flat(flat, SMOOTH_SIZES), split_flat(later, SMOOTH_SIZES))
        )
        shift *= 2
    return flat


def tree_rows(flat, scratch_ref, sizes, combine):
    rows, modes = flat[0].shape
    span = rows
    chunks = modes // 128
    block = len(flat) * span
    while rows > 1:
        half = rows // 2
        for index, value in enumerate(flat):
            for part in range(chunks):
                base = part * block + index * span
                scratch_ref[base:base + rows, :] = value[:, part * 128:(part + 1) * 128]
        even = []
        odd = []
        for index in range(len(flat)):
            pieces_even = []
            pieces_odd = []
            for part in range(chunks):
                base = part * block + index * span
                pieces_even.append(scratch_ref[pl.ds(base, half, stride=2), :])
                pieces_odd.append(scratch_ref[pl.ds(base + 1, half, stride=2), :])
            even.append(jnp.concatenate(pieces_even, axis=1) if chunks > 1 else pieces_even[0])
            odd.append(jnp.concatenate(pieces_odd, axis=1) if chunks > 1 else pieces_odd[0])
        flat = join_flat(combine(split_flat(even, sizes), split_flat(odd, sizes)))
        rows = half
    return flat


def prefix_kernel(elem_ref, out_ref):
    steps = elem_ref.shape[1]
    flat = prefix_rows([elem_ref[index] for index in range(56)], steps // 2)
    for index, value in enumerate(flat):
        out_ref[index] = value


def suffix_kernel(elem_ref, out_ref):
    flat = suffix_rows([elem_ref[index] for index in range(36)])
    for index, value in enumerate(flat):
        out_ref[index] = value


def row_mat(ref):
    return [[ref[4 * r + c:4 * r + c + 1, :] for c in range(4)] for r in range(4)]


def cube_mat(ref):
    return [[ref[r, c:c + 1, :] for c in range(4)] for r in range(4)]


def filter_kernel(
    place_ref, gaps_ref, sensor_ref, obs_ref, seen_ref, noise_ref, read_ref, angle_ref, decay_ref,
    fcov_ref, out_ref, sum_ref, rot_ref, next_ref, scratch_ref,
):
    steps, modes = obs_ref.shape
    total = gaps_ref.shape[0]
    start = place_ref[0] * steps
    row = lax.broadcasted_iota(jnp.int32, (steps, modes), 0)
    zero = jnp.zeros((steps, modes), jnp.float32)
    gap_here = zero
    gap_next = zero
    step_var = zero
    for k in range(steps):
        here = row == k
        gap_here = jnp.where(here, gaps_ref[start + k], gap_here)
        later = jnp.minimum(start + k + 1, total - 1)
        gap_next = jnp.where(here & (start + k + 1 < total), gaps_ref[later], gap_next)
        step_var = jnp.where(here, noise_ref[pl.ds(sensor_ref[k], 1), :], step_var)
    decay = decay_ref[...]
    keep = jnp.where(row + start > 0, jnp.exp(-decay * gap_here), 0.0)
    next_ref[...] = jnp.exp(-decay * gap_next)
    one = jnp.ones((1, modes), jnp.float32)
    flat_zero = jnp.zeros((1, modes), jnp.float32)
    rot = eye4(one, flat_zero)
    planes = ((0, 1), (2, 3), (1, 2), (0, 3))
    for plane_index in range(4):
        first, second = planes[plane_index]
        angle = angle_ref[plane_index:plane_index + 1, :]
        cos_value = jnp.cos(angle)
        sin_value = jnp.sin(angle)
        rotate = eye4(one, flat_zero)
        rotate[first][first] = cos_value
        rotate[second][second] = cos_value
        rotate[first][second] = -sin_value
        rotate[second][first] = sin_value
        rot = mm(rotate, rot)
    for index, value in enumerate(from_mat(rot)):
        rot_ref[index:index + 1, :] = value
    obs = obs_ref[...]
    seen = seen_ref[...].astype(obs.dtype)
    fcov = cube_mat(fcov_ref)
    read = [read_ref[r:r + 1, :] for r in range(4)]
    trans = [[keep * rot[r][c] for c in range(4)] for r in range(4)]
    fade = 1.0 - keep * keep
    noise = [[fade * fcov[r][c] for c in range(4)] for r in range(4)]
    spread = mv(noise, read)
    innov = (
        read[0] * spread[0] + read[1] * spread[1] + read[2] * spread[2] + read[3] * spread[3]
    ) + step_var
    weight = seen / innov
    gain = [weight * spread[r] for r in range(4)]
    shrink = [
        [(1.0 if r == c else 0.0) - gain[r] * read[c] for c in range(4)] for r in range(4)
    ]
    trans_part = mm(shrink, trans)
    offset = [gain[r] * obs for r in range(4)]
    cov_part = [[noise[r][c] - weight * spread[r] * spread[c] for c in range(4)] for r in range(4)]
    pulled = mv(tr(trans), read)
    wy = weight * obs
    vec_part = [wy * pulled[r] for r in range(4)]
    mat_part = [[weight * pulled[r] * pulled[c] for c in range(4)] for r in range(4)]
    flat = join_flat([trans_part, offset, cov_part, vec_part, mat_part])
    for index, value in enumerate(flat):
        out_ref[index] = value
    total_flat = tree_rows(flat, scratch_ref, FILTER_SIZES, filter_combine)
    for index, value in enumerate(total_flat):
        sum_ref[index:index + 1, :] = value


def fold_filter(place, recv_refs):
    count = len(recv_refs) + 1
    mean = None
    cov = None
    for shift in range(count - 1, 0, -1):
        ref = recv_refs[shift - 1]
        element = split_flat([ref[index:index + 1, :] for index in range(56)], FILTER_SIZES)
        if mean is None:
            zero = jnp.zeros_like(element[1][0])
            mean = [zero] * 4
            cov = [[zero] * 4 for _ in range(4)]
        new_mean, new_cov = apply_filter(mean, cov, element)
        take = place >= shift
        mean = [jnp.where(take, a, b) for a, b in zip(new_mean, mean)]
        cov = [[jnp.where(take, a, b) for a, b in zip(ra, rb)] for ra, rb in zip(new_cov, cov)]
    return mean, cov


def fold_smooth(place, recv_refs):
    count = len(recv_refs) + 1
    mean = None
    cov = None
    for shift in range(count - 1, 0, -1):
        ref = recv_refs[shift - 1]
        element = split_flat([ref[index:index + 1, :] for index in range(36)], SMOOTH_SIZES)
        if mean is None:
            zero = jnp.zeros_like(element[1][0])
            mean = [zero] * 4
            cov = [[zero] * 4 for _ in range(4)]
        new_mean, new_cov = apply_smooth(mean, cov, element)
        take = place + shift <= count - 1
        mean = [jnp.where(take, a, b) for a, b in zip(new_mean, mean)]
        cov = [[jnp.where(take, a, b) for a, b in zip(ra, rb)] for ra, rb in zip(new_cov, cov)]
    return mean, cov

def middle_kernel(place_ref, pre_ref, keep_ref, rot_ref, fcov_ref, *rest):
    out_ref, head_ref, scratch_ref = rest[-3:]
    recv_refs = rest[:-3]
    place = place_ref[0]
    enter_mean, enter_cov = fold_filter(place, recv_refs)
    steps = pre_ref.shape[1]
    half = steps // 2
    middle = split_flat([pre_ref[index, half - 1:half, :] for index in range(56)], FILTER_SIZES)
    mid_mean, mid_cov = apply_filter(enter_mean, enter_cov, middle)
    upper = lax.broadcasted_iota(jnp.int32, (steps, pre_ref.shape[2]), 0) < half
    enter_mean = [jnp.where(upper, a, b) for a, b in zip(enter_mean, mid_mean)]
    enter_cov = [[jnp.where(upper, a, b) for a, b in zip(ra, rb)] for ra, rb in zip(enter_cov, mid_cov)]
    element = split_flat([pre_ref[index] for index in range(56)], FILTER_SIZES)
    mean_f, cov_f = apply_filter(enter_mean, enter_cov, element)
    keep = keep_ref[...]
    rot = row_mat(rot_ref)
    fcov = cube_mat(fcov_ref)
    trans = [[keep * rot[r][c] for c in range(4)] for r in range(4)]
    fade = 1.0 - keep * keep
    noise = [[fade * fcov[r][c] for c in range(4)] for r in range(4)]
    trans_t = tr(trans)
    predicted = madd(mm(mm(trans, cov_f), trans_t), noise)
    steps, modes = keep.shape
    row = lax.broadcasted_iota(jnp.int32, (steps, modes), 0)
    count = len(recv_refs) + 1
    live = jnp.where((row == steps - 1) & (place == count - 1), 0.0, 1.0)
    gain = mm(mm(cov_f, trans_t), inv4(predicted))
    gain = [[gain[r][c] * live for c in range(4)] for r in range(4)]
    pushed = mv(gain, mv(trans, mean_f))
    offset = [mean_f[r] - pushed[r] for r in range(4)]
    taken = mm(mm(gain, trans), cov_f)
    resid = [[cov_f[r][c] - taken[r][c] for c in range(4)] for r in range(4)]
    flat = join_flat([gain, offset, resid])
    for index, value in enumerate(flat):
        out_ref[index] = value
    total_flat = tree_rows(flat, scratch_ref, SMOOTH_SIZES, smooth_compose)
    for index, value in enumerate(total_flat):
        head_ref[index:index + 1, :] = value


def final_kernel(place_ref, suf_ref, read_ref, *rest):
    recv_refs = rest[:-2]
    mean_ref, spread_ref = rest[-2:]
    place = place_ref[0]
    leave_mean, leave_cov = fold_smooth(place, recv_refs)
    element = split_flat([suf_ref[index] for index in range(36)], SMOOTH_SIZES)
    mean_s, cov_s = apply_smooth(leave_mean, leave_cov, element)
    read = [read_ref[r:r + 1, :] for r in range(4)]
    for r in range(4):
        mean_ref[:, r, :] = mean_s[r]
    proj = mv(cov_s, read)
    total = read[0] * proj[0] + read[1] * proj[1] + read[2] * proj[2] + read[3] * proj[3]
    spread_ref[...] = jnp.log(total)


def run_kernel(kernel, out_shapes, smem_count, *args, scratch=()):
    specs = [pl.BlockSpec(memory_space=pltpu.SMEM)] * smem_count
    specs += [pl.BlockSpec(memory_space=pltpu.VMEM)] * (len(args) - smem_count)
    return pl.pallas_call(
        kernel, out_shape=out_shapes, in_specs=specs, scratch_shapes=scratch, interpret=INTERPRET
    )(*args)


def rotation_flat(angles):
    mode_count = angles.shape[-1]
    one = jnp.ones((mode_count,), angles.dtype)
    zero = jnp.zeros((mode_count,), angles.dtype)
    result = eye4(one, zero)
    planes = ((0, 1), (2, 3), (1, 2), (0, 3))
    for plane_index in range(4):
        first, second = planes[plane_index]
        cos_value = jnp.cos(angles[plane_index])
        sin_value = jnp.sin(angles[plane_index])
        rotate = eye4(one, zero)
        rotate[first][first] = cos_value
        rotate[second][second] = cos_value
        rotate[first][second] = -sin_value
        rotate[second][first] = sin_value
        result = mm(rotate, result)
    return jnp.stack(from_mat(result), axis=0)


def exchange(summary, forward):
    count = lax.axis_size("tm")
    received = []
    for shift in range(1, count):
        if forward:
            pairs = [(i, (i + shift) % count) for i in range(count)]
        else:
            pairs = [(i, (i - shift) % count) for i in range(count)]
        received.append(lax.ppermute(summary, "tm", pairs))
    return received


def local(
    readings, seen_mask, sensor, time_gaps, noise_var, readout, angles, decay_rates, field_cov
):
    real_type = readings.dtype
    steps_here = readings.shape[0]
    mode_count = readings.shape[1]
    place = jnp.reshape(lax.axis_index("tm"), (1,)).astype(jnp.int32)
    decay = decay_rates.reshape(1, mode_count)
    elements, summary, rot, retain_next = run_kernel(
        filter_kernel,
        (
            jax.ShapeDtypeStruct((56, steps_here, mode_count), real_type),
            jax.ShapeDtypeStruct((56, mode_count), real_type),
            jax.ShapeDtypeStruct((16, mode_count), real_type),
            jax.ShapeDtypeStruct((steps_here, mode_count), real_type),
        ),
        3,
        place, time_gaps, sensor, readings, seen_mask, noise_var, readout, angles, decay, field_cov,
        scratch=[pltpu.VMEM((56 * steps_here * (mode_count // 128), 128), real_type)],
    )
    received = exchange(summary, True)
    prefix = run_kernel(
        prefix_kernel, jax.ShapeDtypeStruct((56, steps_here, mode_count), real_type), 0, elements
    )
    smooth_elems, head = run_kernel(
        middle_kernel,
        (
            jax.ShapeDtypeStruct((36, steps_here, mode_count), real_type),
            jax.ShapeDtypeStruct((36, mode_count), real_type),
        ),
        1,
        place, prefix, retain_next, rot, field_cov, *received,
        scratch=[pltpu.VMEM((36 * steps_here * (mode_count // 128), 128), real_type)],
    )
    received_back = exchange(head, False)
    suffix = run_kernel(
        suffix_kernel, jax.ShapeDtypeStruct((36, steps_here, mode_count), real_type), 0, smooth_elems
    )
    mean_out, log_spread = run_kernel(
        final_kernel,
        (
            jax.ShapeDtypeStruct((steps_here, 4, mode_count), real_type),
            jax.ShapeDtypeStruct((steps_here, mode_count), real_type),
        ),
        1,
        place, suffix, readout, *received_back,
    )
    return (mean_out, log_spread)


def solution(mesh):
    return jax.shard_map(
        local,
        mesh=mesh,
        in_specs=(
            P("tm", "ens"),
            P("tm", None),
            P("tm"),
            P(),
            P(None, "ens"),
            P(None, "ens"),
            P(None, "ens"),
            P("ens"),
            P(None, None, "ens"),
        ),
        out_specs=(P("tm", None, "ens"), P("tm", "ens")),
        check_vma=False,
    )
```
